256 devices in a mesh: gx: 16 (over y, z_lo), gy: 16 (over z_hi, x, core).
Axes of the slice: x: 4, y: 4, z: 8 (z_hi: 2, z_lo: 4; z = z_hi * 4 + z_lo), core: 2. Of those that a mesh axis runs over, the one named last changes fastest.
Arguments:
- vorticity: float32 [8192, 8192], P('gx', 'gy'), may hold values from -6 to 6
- closure_kernel: float32 [3, 3, 3], replicated, may hold values from -1.5 to 1.5
Outputs:
- rate_field: float32 [8192, 8192], P('gx', 'gy')
The draws below stay inside these ranges and needn't reach their ends.
All inputs are finite; a program needn't handle non-finite values.
Results may differ from the reference program's by a relative error of at most 0.0001.
Values sent between devices are 32-bit elements; how exact they have to be, the bound alone decides.
No kernel may reach another device: no remote copies, remote signals or barrier semaphores. Data moves between devices by JAX's collectives and lax.ppermute only.
A program may use at most 128 MiB of HBM per device.

```python
import math
import jax
import jax.numpy as jnp

GRID = 8192


def draw_vorticity(key, part):
    rough_part = jax.random.normal(key, (GRID, GRID), jnp.float32)
    return jnp.clip(rough_part, -6.0, 6.0)


def bell_draw(stream_key, dims, width, most, dtype=jnp.bfloat16):
    values = jax.random.normal(stream_key, dims, jnp.float32) * width
    return jnp.minimum(jnp.maximum(values, -most), most).astype(dtype)


def setup_inputs(seed: int = 0) -> dict:
    arg_keys = jax.random.split(jax.random.key(seed), 3)
    return {
        "vorticity": draw_vorticity(jax.random.fold_in(arg_keys[2], 71), 0),
        "closure_kernel": bell_draw(arg_keys[1], (3, 3, 3), 0.3, 1.5, jnp.float32),
    }


VISCOSITY = 0.5
DRAG = 0.1
FORCE_AMP = 1.0
FORCE_WAVES = 4.0


def transform_speeds(field):
    half_length = GRID // 2
    spectrum = jnp.fft.rfft(field, axis=1)[:, :half_length]
    spectrum = jnp.fft.fft(spectrum, axis=0)
    index_first = jnp.arange(GRID)
    index_first = jnp.where(index_first < half_length, index_first, index_first - GRID)
    number_first = (2.0 * math.pi / GRID) * index_first.astype(jnp.float32)
    number_second = (2.0 * math.pi / GRID) * jnp.arange(half_length).astype(jnp.float32)
    squared = number_first[:, None] ** 2 + number_second[None, :] ** 2
    positive = squared > 0.0
    inverse = jnp.where(positive, 1.0 / jnp.where(positive, squared, 1.0), 0.0)
    potential = spectrum * inverse
    along = 1j * number_second[None, :] * potential
    across = -1j * number_first[:, None] * potential
    speeds = []
    for spectral in (along, across):
        mixed = jnp.fft.ifft(spectral, axis=0)
        mixed = mixed.at[:, 0].set(jnp.real(mixed[:, 0]))
        mixed = jnp.pad(mixed, ((0, 0), (0, 1)))
        speeds.append(jnp.fft.irfft(mixed, n=GRID, axis=1))
    return speeds[0], speeds[1]


def shifted(array, rows_by, cols_by):
    return jnp.roll(array, (rows_by, cols_by), axis=(0, 1))


def rate_of(field, closure_kernel):
    speed_first, speed_second = transform_speeds(field)
    x_minus = shifted(field, 1, 0)
    x_plus = shifted(field, -1, 0)
    y_minus = shifted(field, 0, 1)
    y_plus = shifted(field, 0, -1)
    advect = jnp.maximum(speed_first, 0.0) * (field - x_minus) + jnp.minimum(speed_first, 0.0) * (x_plus - field)
    advect = advect + jnp.maximum(speed_second, 0.0) * (field - y_minus) + jnp.minimum(speed_second, 0.0) * (y_plus - field)
    laplace = x_plus + x_minus + y_plus + y_minus - 4.0 * field
    closure = jnp.zeros_like(field)
    sources = (field, speed_first, speed_second)
    for channel in range(3):
        for shift_row in range(3):
            for shift_col in range(3):
                closure = closure + closure_kernel[channel, shift_row, shift_col] * shifted(sources[channel], 1 - shift_row, 1 - shift_col)
    columns = jnp.arange(GRID).astype(jnp.float32)
    forcing = FORCE_AMP * jnp.cos((2.0 * math.pi * FORCE_WAVES / GRID) * columns)
    return -advect + VISCOSITY * laplace - DRAG * field + forcing[None, :] + closure


def reference(vorticity, closure_kernel):
    return rate_of(vorticity, closure_kernel)
```

```python
import math

import jax
import jax.numpy as jnp
from jax import lax
from jax.sharding import PartitionSpec as P

VISCOSITY = 0.5
DRAG = 0.1
FORCE_AMP = 1.0
FORCE_WAVES = 4.0
EXACT = lax.Precision.HIGHEST
BOTH = ("gx", "gy")


def mm(a, b, dims):
    return lax.dot_general(a, b, (dims, ((), ())), precision=EXACT,
                           preferred_element_type=jnp.float32)


def angle(rows, cols, period):
    idx = (jnp.arange(rows, dtype=jnp.int32)[:, None]
           * jnp.arange(cols, dtype=jnp.int32)[None, :]) % period
    return (2.0 * math.pi / period) * idx.astype(jnp.float32)


def padded(cells, sides, width):
    for axis, dim in sides:
        count = lax.axis_size(axis)
        head = lax.slice_in_dim(cells, 0, width, axis=dim)
        tail = lax.slice_in_dim(cells, cells.shape[dim] - width, cells.shape[dim], axis=dim)
        cells = jnp.concatenate(
            [
                lax.ppermute(tail, axis, [(i, (i + 1) % count) for i in range(count)]),
                cells,
                lax.ppermute(head, axis, [((i + 1) % count, i) for i in range(count)]),
            ],
            axis=dim,
        )
    return cells


def velocity(w):
    g = lax.axis_size("gy")
    bx, by = w.shape
    n = by * g
    r = bx // g
    p = g * g
    k2n = n // 2 // g
    gr = g * r

    a16 = angle(g, g, g)
    fy1 = jnp.concatenate([jnp.cos(a16), -jnp.sin(a16)], axis=0)
    a1 = angle(g, by, n)
    c1, s1 = jnp.cos(a1), -jnp.sin(a1)
    a2 = angle(k2n, by, by)
    cy, sy = jnp.cos(a2), jnp.sin(a2)
    wre = jnp.concatenate([cy, sy], axis=1)
    wim = jnp.concatenate([-sy, cy], axis=1)
    ap = angle(p, p, p)
    fx1 = jnp.concatenate([jnp.cos(ap), jnp.sin(ap)], axis=0)
    at = angle(p, r, n)
    c2 = jnp.tile(jnp.cos(at), (1, g))
    s2 = jnp.tile(jnp.sin(at), (1, g))
    ar = angle(r, r, r)
    eye = jnp.eye(g, dtype=jnp.float32)
    ec = jnp.kron(eye, jnp.cos(ar))
    es = jnp.kron(eye, jnp.sin(ar))
    mfw = jnp.concatenate([jnp.concatenate([ec, -es], axis=1),
                           jnp.concatenate([es, ec], axis=1)], axis=0)
    mbw = jnp.concatenate([jnp.concatenate([ec, es], axis=1),
                           jnp.concatenate([-es, ec], axis=1)], axis=0)
    a3 = angle(g, g, g)
    fy3 = jnp.concatenate([jnp.cos(a3), -jnp.sin(a3)], axis=1)

    rows = lax.all_to_all(w.reshape(g, r, by), "gy", 0, 0, tiled=True)
    t = mm(fy1, rows.reshape(g, r * by), ((1,), (0,))).reshape(2, g, r, by)
    tre = t[0] * c1[:, None, :] - t[1] * s1[:, None, :]
    tim = t[0] * s1[:, None, :] + t[1] * c1[:, None, :]
    tcat = jnp.concatenate([tre, tim], axis=-1).reshape(gr, 2 * by)
    wr = mm(wre, tcat, ((1,), (1,)))
    wi = mm(wim, tcat, ((1,), (1,)))
    wcat = jnp.concatenate([wr, wi], axis=1)

    dx = lax.all_to_all(wcat, BOTH, 0, 0, tiled=True)
    z = mm(fx1, dx, ((1,), (0,)))
    z0, z1 = z[:p], z[p:]
    yre = z0[:, :gr] + z1[:, gr:]
    yim = z0[:, gr:] - z1[:, :gr]
    ycat = jnp.concatenate([yre * c2 + yim * s2, yim * c2 - yre * s2], axis=1)
    xh = mm(ycat, mfw, ((1,), (0,)))

    me = lax.axis_index("gx") * g + lax.axis_index("gy")
    col = jnp.arange(gr, dtype=jnp.int32)[None, :]
    k1x = jnp.arange(p, dtype=jnp.int32)[:, None]
    mx = k1x + p * (col % r)
    mx = jnp.where(mx < n // 2, mx, mx - n)
    ky_i = (col // r) % g + g * me
    kx = (2.0 * math.pi / n) * mx.astype(jnp.float32)
    ky = (2.0 * math.pi / n) * ky_i.astype(jnp.float32)
    sq = kx * kx + ky * ky
    pos = sq > 0.0
    inv = jnp.where(pos, 1.0 / jnp.where(pos, sq, 1.0), 0.0)
    weight = jnp.where(ky_i == 0, 1.0, 2.0) * (1.0 / (float(n) * float(n)))
    pre = xh[:, :gr] * inv
    pim = xh[:, gr:] * inv
    fu = ky * weight
    fv = kx * weight
    spec = jnp.concatenate([
        jnp.concatenate([-fu * pim, fu * pre], axis=1),
        jnp.concatenate([fv * pim, -fv * pre], axis=1),
    ], axis=0)

    q = mm(spec, mbw, ((1,), (0,)))
    qre, qim = q[:, :gr], q[:, gr:]
    c2b = jnp.concatenate([c2, c2], axis=0)
    s2b = jnp.concatenate([s2, s2], axis=0)
    qre2 = qre * c2b - qim * s2b
    qim2 = qre * s2b + qim * c2b
    qcat = jnp.concatenate([qre2[:p], qim2[:p], qre2[p:], qim2[p:]], axis=1)
    zb = mm(fx1, qcat, ((1,), (0,)))
    zb0, zb1 = zb[:p], zb[p:]
    parts = []
    for f in range(2):
        o = 2 * f * gr
        parts.append(zb0[:, o:o + gr] - zb1[:, o + gr:o + 2 * gr])
        parts.append(zb0[:, o + gr:o + 2 * gr] + zb1[:, o:o + gr])
    scat = jnp.concatenate(parts, axis=1)

    ey = lax.all_to_all(scat, BOTH, 0, 0, tiled=True)
    zz = mm(ey, wre, ((0,), (0,))).reshape(2, 2, g, r, 2 * by)
    vre = zz[:, 0, :, :, :by] - zz[:, 1, :, :, by:]
    vim = zz[:, 0, :, :, by:] + zz[:, 1, :, :, :by]
    vre2 = vre * c1[None, :, None, :] + vim * s1[None, :, None, :]
    vim2 = vim * c1[None, :, None, :] - vre * s1[None, :, None, :]
    vst = jnp.concatenate([vre2, vim2], axis=1).reshape(2, 2 * g, r * by)
    uv = mm(fy3, vst, ((1,), (1,))).reshape(g, 2, r, by)
    back = lax.all_to_all(uv, "gy", 0, 0, tiled=True)
    u = back[:, 0].reshape(bx, by)
    v = back[:, 1].reshape(bx, by)
    return u, v, n


def tendency(extended, closure_kernel, column_start, n):
    vortex = extended[0]
    centre = vortex[1:-1, 1:-1]
    rows_count = centre.shape[0]
    cols_count = centre.shape[1]
    x_minus = vortex[:-2, 1:-1]
    x_plus = vortex[2:, 1:-1]
    y_minus = vortex[1:-1, :-2]
    y_plus = vortex[1:-1, 2:]
    speed_first = extended[1, 1:-1, 1:-1]
    speed_second = extended[2, 1:-1, 1:-1]
    advect = jnp.maximum(speed_first, 0.0) * (centre - x_minus) + jnp.minimum(speed_first, 0.0) * (
        x_plus - centre
    )
    advect = (
        advect
        + jnp.maximum(speed_second, 0.0) * (centre - y_minus)
        + jnp.minimum(speed_second, 0.0) * (y_plus - centre)
    )
    laplace = x_plus + x_minus + y_plus + y_minus - 4.0 * centre
    closure = jnp.zeros_like(centre)
    for channel in range(3):
        for shift_row in range(3):
            for shift_col in range(3):
                closure = (
                    closure
                    + closure_kernel[channel, shift_row, shift_col]
                    * extended[
                        channel,
                        shift_row : shift_row + rows_count,
                        shift_col : shift_col + cols_count,
                    ]
                )
    columns = (column_start + jnp.arange(cols_count, dtype=jnp.int32)).astype(jnp.float32)
    forcing = FORCE_AMP * jnp.cos(2.0 * math.pi * FORCE_WAVES / n * columns)
    return -advect + VISCOSITY * laplace - DRAG * centre + forcing[None, :] + closure


def per_device(vorticity, closure_kernel):
    u, v, n = velocity(vorticity)
    stacked = jnp.stack([vorticity, u, v], axis=0)
    extended = padded(stacked, (("gx", 1), ("gy", 2)), 1)
    return tendency(extended, closure_kernel, lax.axis_index("gy") * vorticity.shape[1], n)


def solution(mesh):
    placed = (P("gx", "gy"), P())
    return jax.shard_map(
        per_device, mesh=mesh, in_specs=placed, out_specs=P("gx", "gy"), check_vma=False
    )
```

```python
import math

import jax
import jax.numpy as jnp
from jax import lax
from jax.sharding import PartitionSpec as P
from jax.experimental import pallas as pl
from jax.experimental.pallas import tpu as pltpu

VISCOSITY = 0.5
DRAG = 0.1
FORCE_AMP = 1.0
FORCE_WAVES = 4.0
EXACT = lax.Precision.HIGHEST
BOTH = ("gx", "gy")


def mm(a, b, dims):
    return lax.dot_general(a, b, (dims, ((), ())), precision=EXACT,
                           preferred_element_type=jnp.float32)


def angle(rows, cols, period):
    idx = (jnp.arange(rows, dtype=jnp.int32)[:, None]
           * jnp.arange(cols, dtype=jnp.int32)[None, :]) % period
    return (2.0 * math.pi / period) * idx.astype(jnp.float32)


def padded(cells, sides, width):
    for axis, dim in sides:
        count = lax.axis_size(axis)
        head = lax.slice_in_dim(cells, 0, width, axis=dim)
        tail = lax.slice_in_dim(cells, cells.shape[dim] - width, cells.shape[dim], axis=dim)
        cells = jnp.concatenate(
            [
                lax.ppermute(tail, axis, [(i, (i + 1) % count) for i in range(count)]),
                cells,
                lax.ppermute(head, axis, [((i + 1) % count, i) for i in range(count)]),
            ],
            axis=dim,
        )
    return cells


def velocity(w):
    g = lax.axis_size("gy")
    bx, by = w.shape
    n = by * g
    r = bx // g
    p = g * g
    k2n = n // 2 // g
    gr = g * r

    a16 = angle(g, g, g)
    fy1 = jnp.concatenate([jnp.cos(a16), -jnp.sin(a16)], axis=0)
    a1 = angle(g, by, n)
    c1, s1 = jnp.cos(a1), -jnp.sin(a1)
    a2 = angle(k2n, by, by)
    cy, sy = jnp.cos(a2), jnp.sin(a2)
    wre = jnp.concatenate([cy, sy], axis=1)
    wim = jnp.concatenate([-sy, cy], axis=1)
    ap = angle(p, p, p)
    fx1 = jnp.concatenate([jnp.cos(ap), jnp.sin(ap)], axis=0)
    at = angle(p, r, n)
    c2 = jnp.tile(jnp.cos(at), (1, g))
    s2 = jnp.tile(jnp.sin(at), (1, g))
    ar = angle(r, r, r)
    eye = jnp.eye(g, dtype=jnp.float32)
    ec = jnp.kron(eye, jnp.cos(ar))
    es = jnp.kron(eye, jnp.sin(ar))
    mfw = jnp.concatenate([jnp.concatenate([ec, -es], axis=1),
                           jnp.concatenate([es, ec], axis=1)], axis=0)
    mbw = jnp.concatenate([jnp.concatenate([ec, es], axis=1),
                           jnp.concatenate([-es, ec], axis=1)], axis=0)
    a3 = angle(g, g, g)
    fy3 = jnp.concatenate([jnp.cos(a3), -jnp.sin(a3)], axis=1)

    rows = lax.all_to_all(w.reshape(g, r, by), "gy", 0, 0, tiled=True)
    t = mm(fy1, rows.reshape(g, r * by), ((1,), (0,))).reshape(2, g, r, by)
    tre = t[0] * c1[:, None, :] - t[1] * s1[:, None, :]
    tim = t[0] * s1[:, None, :] + t[1] * c1[:, None, :]
    tcat = jnp.concatenate([tre, tim], axis=-1).reshape(gr, 2 * by)
    wr = mm(wre, tcat, ((1,), (1,)))
    wi = mm(wim, tcat, ((1,), (1,)))
    wcat = jnp.concatenate([wr, wi], axis=1)

    dx = lax.all_to_all(wcat, BOTH, 0, 0, tiled=True)
    z = mm(fx1, dx, ((1,), (0,)))
    z0, z1 = z[:p], z[p:]
    yre = z0[:, :gr] + z1[:, gr:]
    yim = z0[:, gr:] - z1[:, :gr]
    ycat = jnp.concatenate([yre * c2 + yim * s2, yim * c2 - yre * s2], axis=1)
    xh = mm(ycat, mfw, ((1,), (0,)))

    me = lax.axis_index("gx") * g + lax.axis_index("gy")
    col = jnp.arange(gr, dtype=jnp.int32)[None, :]
    k1x = jnp.arange(p, dtype=jnp.int32)[:, None]
    mx = k1x + p * (col % r)
    mx = jnp.where(mx < n // 2, mx, mx - n)
    ky_i = (col // r) % g + g * me
    kx = (2.0 * math.pi / n) * mx.astype(jnp.float32)
    ky = (2.0 * math.pi / n) * ky_i.astype(jnp.float32)
    sq = kx * kx + ky * ky
    pos = sq > 0.0
    inv = jnp.where(pos, 1.0 / jnp.where(pos, sq, 1.0), 0.0)
    weight = jnp.where(ky_i == 0, 1.0, 2.0) * (1.0 / (float(n) * float(n)))
    pre = xh[:, :gr] * inv
    pim = xh[:, gr:] * inv
    fu = ky * weight
    fv = kx * weight
    spec = jnp.concatenate([
        jnp.concatenate([-fu * pim, fu * pre], axis=1),
        jnp.concatenate([fv * pim, -fv * pre], axis=1),
    ], axis=0)

    q = mm(spec, mbw, ((1,), (0,)))
    qre, qim = q[:, :gr], q[:, gr:]
    c2b = jnp.concatenate([c2, c2], axis=0)
    s2b = jnp.concatenate([s2, s2], axis=0)
    qre2 = qre * c2b - qim * s2b
    qim2 = qre * s2b + qim * c2b
    qcat = jnp.concatenate([qre2[:p], qim2[:p], qre2[p:], qim2[p:]], axis=1)
    zb = mm(fx1, qcat, ((1,), (0,)))
    zb0, zb1 = zb[:p], zb[p:]
    parts = []
    for f in range(2):
        o = 2 * f * gr
        parts.append(zb0[:, o:o + gr] - zb1[:, o + gr:o + 2 * gr])
        parts.append(zb0[:, o + gr:o + 2 * gr] + zb1[:, o:o + gr])
    scat = jnp.concatenate(parts, axis=1)

    ey = lax.all_to_all(scat, BOTH, 0, 0, tiled=True)
    zz = mm(ey, wre, ((0,), (0,))).reshape(2, 2, g, r, 2 * by)
    vre = zz[:, 0, :, :, :by] - zz[:, 1, :, :, by:]
    vim = zz[:, 0, :, :, by:] + zz[:, 1, :, :, :by]
    vre2 = vre * c1[None, :, None, :] + vim * s1[None, :, None, :]
    vim2 = vim * c1[None, :, None, :] - vre * s1[None, :, None, :]
    vst = jnp.concatenate([vre2, vim2], axis=1).reshape(2, 2 * g, r * by)
    uv = mm(fy3, vst, ((1,), (1,))).reshape(g, 2, r, by)
    back = lax.all_to_all(uv, "gy", 0, 0, tiled=True)
    u = back[:, 0].reshape(bx, by)
    v = back[:, 1].reshape(bx, by)
    return u, v, n


def rate_kernel(k_ref, ext_ref, frc_ref, out_ref):
    rows, cols = ext_ref.shape[1], ext_ref.shape[2]
    bx, by = out_ref.shape

    def rr(a, s):
        return pltpu.roll(a, s % rows, 0)

    def lr(a, s):
        return pltpu.roll(a, s % cols, 1)

    w = ext_ref[0]
    u = ext_ref[1]
    v = ext_ref[2]
    wm = rr(w, 1)
    wp = rr(w, -1)
    ym = lr(w, 1)
    yp = lr(w, -1)
    adv = (jnp.maximum(u, 0.0) * (w - wm) + jnp.minimum(u, 0.0) * (wp - w)
           + jnp.maximum(v, 0.0) * (w - ym) + jnp.minimum(v, 0.0) * (yp - w))
    lap = wp + wm + yp + ym - 4.0 * w
    g = [None, None, None]
    for c, f in enumerate((w, u, v)):
        fm = wm if c == 0 else rr(f, 1)
        fp = wp if c == 0 else rr(f, -1)
        for b in range(3):
            term = (k_ref[9 * c + b] * fm + k_ref[9 * c + 3 + b] * f
                    + k_ref[9 * c + 6 + b] * fp)
            g[b] = term if g[b] is None else g[b] + term
    clo = g[1] + lr(g[0], 1) + lr(g[2], -1)
    res = -adv + VISCOSITY * lap - DRAG * w + clo
    res = rr(lr(res, -1), -1)
    out_ref[...] = res[:bx, :by] + frc_ref[0:1, :]


def rate_field(extended, closure_kernel, column_start, n):
    _, ex, ey = extended.shape
    bx, by = ex - 2, ey - 2
    rows = -(-ex // 8) * 8
    cols = -(-ey // 128) * 128
    ext = jnp.pad(extended, ((0, 0), (0, rows - ex), (0, cols - ey)))
    columns = (column_start + jnp.arange(by, dtype=jnp.int32)).astype(jnp.float32)
    forcing = FORCE_AMP * jnp.cos(2.0 * math.pi * FORCE_WAVES / n * columns)
    frc = jnp.broadcast_to(forcing[None, :], (8, by))
    return pl.pallas_call(
        rate_kernel,
        out_shape=jax.ShapeDtypeStruct((bx, by), jnp.float32),
        in_specs=[
            pl.BlockSpec(memory_space=pltpu.SMEM),
            pl.BlockSpec(memory_space=pltpu.VMEM),
            pl.BlockSpec(memory_space=pltpu.VMEM),
        ],
        out_specs=pl.BlockSpec(memory_space=pltpu.VMEM),
        compiler_params=pltpu.CompilerParams(vmem_limit_bytes=60 * 1024 * 1024),
        cost_estimate=pl.CostEstimate(flops=60 * rows * cols, transcendentals=0,
                                      bytes_accessed=4 * (3 * rows * cols + bx * by)),
    )(closure_kernel.reshape(-1), ext, frc)


def per_device(vorticity, closure_kernel):
    w_ext = padded(vorticity[None], (("gx", 1), ("gy", 2)), 1)
    u, v, n = velocity(vorticity)
    uv_ext = padded(jnp.stack([u, v], axis=0), (("gx", 1), ("gy", 2)), 1)
    extended = jnp.concatenate([w_ext, uv_ext], axis=0)
    return rate_field(extended, closure_kernel, lax.axis_index("gy") * vorticity.shape[1], n)


def solution(mesh):
    placed = (P("gx", "gy"), P())
    return jax.shard_map(
        per_device, mesh=mesh, in_specs=placed, out_specs=P("gx", "gy"), check_vma=False
    )
```

```python
import math

import jax
import jax.numpy as jnp
from jax import lax
from jax.sharding import PartitionSpec as P
from jax.experimental import pallas as pl
from jax.experimental.pallas import tpu as pltpu

VISCOSITY = 0.5
DRAG = 0.1
FORCE_AMP = 1.0
FORCE_WAVES = 4.0
EXACT = lax.Precision.HIGHEST
BOTH = ("gx", "gy")


def mm(a, b, dims):
    return lax.dot_general(a, b, (dims, ((), ())), precision=EXACT,
                           preferred_element_type=jnp.float32)


def angle(rows, cols, period):
    idx = (jnp.arange(rows, dtype=jnp.int32)[:, None]
           * jnp.arange(cols, dtype=jnp.int32)[None, :]) % period
    return (2.0 * math.pi / period) * idx.astype(jnp.float32)


def velocity(w):
    g = lax.axis_size("gy")
    bx, by = w.shape
    n = by * g
    r = bx // g
    p = g * g
    k2n = n // 2 // g
    gr = g * r

    a16 = angle(g, g, g)
    fy1 = jnp.concatenate([jnp.cos(a16), -jnp.sin(a16)], axis=0)
    a1 = angle(g, by, n)
    c1, s1 = jnp.cos(a1), -jnp.sin(a1)
    a2 = angle(k2n, by, by)
    cy, sy = jnp.cos(a2), jnp.sin(a2)
    wre = jnp.concatenate([cy, sy], axis=1)
    wim = jnp.concatenate([-sy, cy], axis=1)
    ap = angle(p, p, p)
    fx1 = jnp.concatenate([jnp.cos(ap), jnp.sin(ap)], axis=0)
    at = angle(p, r, n)
    c2 = jnp.tile(jnp.cos(at), (1, g))
    s2 = jnp.tile(jnp.sin(at), (1, g))
    ar = angle(r, r, r)
    eye = jnp.eye(g, dtype=jnp.float32)
    ec = jnp.kron(eye, jnp.cos(ar))
    es = jnp.kron(eye, jnp.sin(ar))
    mfw = jnp.concatenate([jnp.concatenate([ec, -es], axis=1),
                           jnp.concatenate([es, ec], axis=1)], axis=0)
    mbw = jnp.concatenate([jnp.concatenate([ec, es], axis=1),
                           jnp.concatenate([-es, ec], axis=1)], axis=0)
    a3 = angle(g, g, g)
    fy3 = jnp.concatenate([jnp.cos(a3), -jnp.sin(a3)], axis=1)

    rows = lax.all_to_all(w.reshape(g, r, by), "gy", 0, 0, tiled=True)
    t = mm(fy1, rows.reshape(g, r * by), ((1,), (0,))).reshape(2, g, r, by)
    tre = t[0] * c1[:, None, :] - t[1] * s1[:, None, :]
    tim = t[0] * s1[:, None, :] + t[1] * c1[:, None, :]
    tcat = jnp.concatenate([tre, tim], axis=-1).reshape(gr, 2 * by)
    wr = mm(wre, tcat, ((1,), (1,)))
    wi = mm(wim, tcat, ((1,), (1,)))
    wcat = jnp.concatenate([wr, wi], axis=1)

    dx = lax.all_to_all(wcat, BOTH, 0, 0, tiled=True)
    z = mm(fx1, dx, ((1,), (0,)))
    z0, z1 = z[:p], z[p:]
    yre = z0[:, :gr] + z1[:, gr:]
    yim = z0[:, gr:] - z1[:, :gr]
    ycat = jnp.concatenate([yre * c2 + yim * s2, yim * c2 - yre * s2], axis=1)
    xh = mm(ycat, mfw, ((1,), (0,)))

    me = lax.axis_index("gx") * g + lax.axis_index("gy")
    col = jnp.arange(gr, dtype=jnp.int32)[None, :]
    k1x = jnp.arange(p, dtype=jnp.int32)[:, None]
    mx = k1x + p * (col % r)
    mx = jnp.where(mx < n // 2, mx, mx - n)
    ky_i = (col // r) % g + g * me
    kx = (2.0 * math.pi / n) * mx.astype(jnp.float32)
    ky = (2.0 * math.pi / n) * ky_i.astype(jnp.float32)
    sq = kx * kx + ky * ky
    pos = sq > 0.0
    inv = jnp.where(pos, 1.0 / jnp.where(pos, sq, 1.0), 0.0)
    weight = jnp.where(ky_i == 0, 1.0, 2.0) * (1.0 / (float(n) * float(n)))
    pre = xh[:, :gr] * inv
    pim = xh[:, gr:] * inv
    fu = ky * weight
    fv = kx * weight
    spec = jnp.concatenate([
        jnp.concatenate([-fu * pim, fu * pre], axis=1),
        jnp.concatenate([fv * pim, -fv * pre], axis=1),
    ], axis=0)

    q = mm(spec, mbw, ((1,), (0,)))
    qre, qim = q[:, :gr], q[:, gr:]
    c2b = jnp.concatenate([c2, c2], axis=0)
    s2b = jnp.concatenate([s2, s2], axis=0)
    qre2 = qre * c2b - qim * s2b
    qim2 = qre * s2b + qim * c2b
    qcat = jnp.concatenate([qre2[:p], qim2[:p], qre2[p:], qim2[p:]], axis=1)
    zb = mm(fx1, qcat, ((1,), (0,)))
    zb0, zb1 = zb[:p], zb[p:]
    parts = []
    for f in range(2):
        o = 2 * f * gr
        parts.append(zb0[:, o:o + gr] - zb1[:, o + gr:o + 2 * gr])
        parts.append(zb0[:, o + gr:o + 2 * gr] + zb1[:, o:o + gr])
    scat = jnp.concatenate(parts, axis=1)

    ey = lax.all_to_all(scat, BOTH, 0, 0, tiled=True)
    zz = mm(ey, wre, ((0,), (0,))).reshape(2, 2, g, r, 2 * by)
    vre = zz[:, 0, :, :, :by] - zz[:, 1, :, :, by:]
    vim = zz[:, 0, :, :, by:] + zz[:, 1, :, :, :by]
    vre2 = vre * c1[None, :, None, :] + vim * s1[None, :, None, :]
    vim2 = vim * c1[None, :, None, :] - vre * s1[None, :, None, :]
    vst = jnp.concatenate([vre2, vim2], axis=1).reshape(2, 2 * g, r * by)
    uv = mm(fy3, vst, ((1,), (1,))).reshape(g, 2, r, by)
    back = lax.all_to_all(uv, "gy", 0, 0, tiled=True)
    return back, n


def rate_kernel(k_ref, w_ref, back_ref, bot_ref, side_ref, frc_ref, out_ref, ext_ref):
    rows, cols = ext_ref.shape[1], ext_ref.shape[2]
    bx, by = out_ref.shape
    g, _, r, _ = back_ref.shape

    ext_ref[0, :bx, :by] = w_ref[...]
    for f in range(2):
        for j in range(g):
            ext_ref[1 + f, j * r:(j + 1) * r, :by] = back_ref[j, f]
    for c in range(3):
        ext_ref[c, bx:, :] = bot_ref[c]
        ext_ref[c, :bx, by:] = side_ref[c]

    def rr(a, s):
        return pltpu.roll(a, s % rows, 0)

    def lr(a, s):
        return pltpu.roll(a, s % cols, 1)

    w = ext_ref[0]
    u = ext_ref[1]
    v = ext_ref[2]
    wm = rr(w, 1)
    wp = rr(w, -1)
    ym = lr(w, 1)
    yp = lr(w, -1)
    adv = (jnp.maximum(u, 0.0) * (w - wm) + jnp.minimum(u, 0.0) * (wp - w)
           + jnp.maximum(v, 0.0) * (w - ym) + jnp.minimum(v, 0.0) * (yp - w))
    lap = wp + wm + yp + ym - 4.0 * w
    gs = [None, None, None]
    for c, f in enumerate((w, u, v)):
        fm = wm if c == 0 else rr(f, 1)
        fp = wp if c == 0 else rr(f, -1)
        for b in range(3):
            term = (k_ref[9 * c + b] * fm + k_ref[9 * c + 3 + b] * f
                    + k_ref[9 * c + 6 + b] * fp)
            gs[b] = term if gs[b] is None else gs[b] + term
    clo = gs[1] + lr(gs[0], 1) + lr(gs[2], -1)
    res = -adv + VISCOSITY * lap - DRAG * w + clo
    out_ref[...] = res[:bx, :by] + frc_ref[0:1, :]


def halo(top, bottom, left, right, corners):
    gx, gy = lax.axis_size("gx"), lax.axis_size("gy")

    def shift(x, axis, count, step):
        return lax.ppermute(x, axis, [(i, (i + step) % count) for i in range(count)])

    def diag(x, di, dj):
        pairs = []
        for i in range(gx):
            for j in range(gy):
                pairs.append((i * gy + j, ((i + di) % gx) * gy + (j + dj) % gy))
        return lax.ppermute(x, BOTH, pairs)

    below = shift(top, "gx", gx, -1)
    above = shift(bottom, "gx", gx, 1)
    after = shift(left, "gy", gy, -1)
    before = shift(right, "gy", gy, 1)
    c_br = diag(corners[:, 0], -1, -1)
    c_bl = diag(corners[:, 1], -1, 1)
    c_tr = diag(corners[:, 2], 1, -1)
    c_tl = diag(corners[:, 3], 1, 1)
    return below, above, after, before, c_br, c_bl, c_tr, c_tl


def strips(parts, bx, by, rows, cols):
    below, above, after, before, c_br, c_bl, c_tr, c_tl = parts
    nc = below.shape[0]
    ri = jnp.arange(rows - bx, dtype=jnp.int32)[:, None]
    ci = jnp.arange(cols, dtype=jnp.int32)[None, :]
    pad = cols - by
    row_lo = jnp.concatenate([below, c_br[:, None], jnp.zeros((nc, pad - 2)), c_bl[:, None]], axis=1)
    row_hi = jnp.concatenate([above, c_tr[:, None], jnp.zeros((nc, pad - 2)), c_tl[:, None]], axis=1)
    bot = jnp.where(ri[None] == 0, row_lo[:, None, :],
                    jnp.where(ri[None] == rows - bx - 1, row_hi[:, None, :], 0.0))
    si = jnp.arange(pad, dtype=jnp.int32)[None, None, :]
    side = jnp.where(si == 0, after[:, :, None], jnp.where(si == pad - 1, before[:, :, None], 0.0))
    return bot, side


def per_device(vorticity, closure_kernel):
    bx, by = vorticity.shape
    rows = -(-(bx + 2) // 8) * 8
    cols = -(-(by + 2) // 128) * 128
    w = vorticity
    w_parts = halo(w[None, 0], w[None, -1], w[None, :, 0], w[None, :, -1],
                   jnp.stack([w[0, 0], w[0, -1], w[-1, 0], w[-1, -1]])[None])
    back, n = velocity(vorticity)
    uv_top = back[0, :, 0, :]
    uv_bot = back[-1, :, -1, :]
    uv_left = jnp.transpose(back[:, :, :, 0], (1, 0, 2)).reshape(2, bx)
    uv_right = jnp.transpose(back[:, :, :, -1], (1, 0, 2)).reshape(2, bx)
    uv_corn = jnp.stack([uv_top[:, 0], uv_top[:, -1], uv_bot[:, 0], uv_bot[:, -1]], axis=1)
    uv_parts = halo(uv_top, uv_bot, uv_left, uv_right, uv_corn)
    parts = [jnp.concatenate([a, b], axis=0) for a, b in zip(w_parts, uv_parts)]
    bot, side = strips(parts, bx, by, rows, cols)
    columns = (lax.axis_index("gy") * by + jnp.arange(by, dtype=jnp.int32)).astype(jnp.float32)
    forcing = FORCE_AMP * jnp.cos(2.0 * math.pi * FORCE_WAVES / n * columns)
    frc = jnp.broadcast_to(forcing[None, :], (8, by))
    return pl.pallas_call(
        rate_kernel,
        out_shape=jax.ShapeDtypeStruct((bx, by), jnp.float32),
        in_specs=[pl.BlockSpec(memory_space=pltpu.SMEM)]
        + [pl.BlockSpec(memory_space=pltpu.VMEM)] * 5,
        out_specs=pl.BlockSpec(memory_space=pltpu.VMEM),
        scratch_shapes=[pltpu.VMEM((3, rows, cols), jnp.float32)],
        compiler_params=pltpu.CompilerParams(vmem_limit_bytes=60 * 1024 * 1024),
        cost_estimate=pl.CostEstimate(flops=60 * rows * cols, transcendentals=0,
                                      bytes_accessed=4 * (4 * rows * cols)),
    )(closure_kernel.reshape(-1), w, back, bot, side, frc)


def solution(mesh):
    placed = (P("gx", "gy"), P())
    return jax.shard_map(
        per_device, mesh=mesh, in_specs=placed, out_specs=P("gx", "gy"), check_vma=False
    )
```

```python
import math

import jax
import jax.numpy as jnp
from jax import lax
from jax.sharding import PartitionSpec as P
from jax.experimental import pallas as pl
from jax.experimental.pallas import tpu as pltpu

VISCOSITY = 0.5
DRAG = 0.1
FORCE_AMP = 1.0
FORCE_WAVES = 4.0
EXACT = lax.Precision.HIGHEST
BOTH = ("gx", "gy")


def mm(a, b, dims):
    return lax.dot_general(a, b, (dims, ((), ())), precision=EXACT,
                           preferred_element_type=jnp.float32)


def angle(rows, cols, period):
    idx = (jnp.arange(rows, dtype=jnp.int32)[:, None]
           * jnp.arange(cols, dtype=jnp.int32)[None, :]) % period
    return (2.0 * math.pi / period) * idx.astype(jnp.float32)


def velocity(w):
    g = lax.axis_size("gy")
    bx, by = w.shape
    n = by * g
    r = bx // g
    p = g * g
    k2n = n // 2 // g
    gr = g * r

    a16 = angle(g, g, g)
    fy1 = jnp.concatenate([jnp.cos(a16), -jnp.sin(a16)], axis=0)
    a1 = angle(g, by, n)
    c1, s1 = jnp.cos(a1), -jnp.sin(a1)
    a2 = angle(k2n, by, by)
    cy, sy = jnp.cos(a2), jnp.sin(a2)
    wre = jnp.concatenate([cy, sy], axis=1)
    wim = jnp.concatenate([-sy, cy], axis=1)
    ap = angle(p, p, p)
    fx1 = jnp.concatenate([jnp.cos(ap), jnp.sin(ap)], axis=0)
    at = angle(p, r, n)
    c2 = jnp.tile(jnp.cos(at), (1, g))
    s2 = jnp.tile(jnp.sin(at), (1, g))
    ar = angle(r, r, r)
    eye = jnp.eye(g, dtype=jnp.float32)
    ec = jnp.kron(eye, jnp.cos(ar))
    es = jnp.kron(eye, jnp.sin(ar))
    mfw = jnp.concatenate([jnp.concatenate([ec, -es], axis=1),
                           jnp.concatenate([es, ec], axis=1)], axis=0)
    mbw = jnp.concatenate([jnp.concatenate([ec, es], axis=1),
                           jnp.concatenate([-es, ec], axis=1)], axis=0)
    a3 = angle(g, g, g)
    fy3 = jnp.concatenate([jnp.cos(a3), -jnp.sin(a3)], axis=1)

    rows = lax.all_to_all(w.reshape(g, r, by), "gy", 0, 0, tiled=True)
    t = mm(fy1, rows.reshape(g, r * by), ((1,), (0,))).reshape(2, g, r, by)
    tre = t[0] * c1[:, None, :] - t[1] * s1[:, None, :]
    tim = t[0] * s1[:, None, :] + t[1] * c1[:, None, :]
    tcat = jnp.concatenate([tre, tim], axis=-1).reshape(gr, 2 * by)
    wr = mm(wre, tcat, ((1,), (1,)))
    wi = mm(wim, tcat, ((1,), (1,)))
    wcat = jnp.concatenate([wr, wi], axis=1)

    dx = lax.all_to_all(wcat, BOTH, 0, 0, tiled=True)
    z = mm(fx1, dx, ((1,), (0,)))
    z0, z1 = z[:p], z[p:]
    yre = z0[:, :gr] + z1[:, gr:]
    yim = z0[:, gr:] - z1[:, :gr]
    ycat = jnp.concatenate([yre * c2 + yim * s2, yim * c2 - yre * s2], axis=1)
    xh = mm(ycat, mfw, ((1,), (0,)))

    me = lax.axis_index("gx") * g + lax.axis_index("gy")
    col = jnp.arange(gr, dtype=jnp.int32)[None, :]
    k1x = jnp.arange(p, dtype=jnp.int32)[:, None]
    mx = k1x + p * (col % r)
    mx = jnp.where(mx < n // 2, mx, mx - n)
    ky_i = (col // r) % g + g * me
    kx = (2.0 * math.pi / n) * mx.astype(jnp.float32)
    ky = (2.0 * math.pi / n) * ky_i.astype(jnp.float32)
    sq = kx * kx + ky * ky
    pos = sq > 0.0
    inv = jnp.where(pos, 1.0 / jnp.where(pos, sq, 1.0), 0.0)
    weight = jnp.where(ky_i == 0, 1.0, 2.0) * (1.0 / (float(n) * float(n)))
    pre = xh[:, :gr] * inv
    pim = xh[:, gr:] * inv
    fu = ky * weight
    fv = kx * weight
    spec = jnp.concatenate([
        jnp.concatenate([-fu * pim, fu * pre], axis=1),
        jnp.concatenate([fv * pim, -fv * pre], axis=1),
    ], axis=0)

    q = mm(spec, mbw, ((1,), (0,)))
    qre, qim = q[:, :gr], q[:, gr:]
    c2b = jnp.concatenate([c2, c2], axis=0)
    s2b = jnp.concatenate([s2, s2], axis=0)
    qre2 = qre * c2b - qim * s2b
    qim2 = qre * s2b + qim * c2b
    qcat = jnp.concatenate([qre2[:p], qim2[:p], qre2[p:], qim2[p:]], axis=1)
    zb = mm(fx1, qcat, ((1,), (0,)))
    zb0, zb1 = zb[:p], zb[p:]
    parts = []
    for f in range(2):
        o = 2 * f * gr
        parts.append(zb0[:, o:o + gr] - zb1[:, o + gr:o + 2 * gr])
        parts.append(zb0[:, o + gr:o + 2 * gr] + zb1[:, o:o + gr])
    scat = jnp.concatenate(parts, axis=1)

    ey = lax.all_to_all(scat, BOTH, 0, 0, tiled=True)
    zz = mm(ey, wre, ((0,), (0,))).reshape(2, 2, g, r, 2 * by)
    vre = zz[:, 0, :, :, :by] - zz[:, 1, :, :, by:]
    vim = zz[:, 0, :, :, by:] + zz[:, 1, :, :, :by]
    vre2 = vre * c1[None, :, None, :] + vim * s1[None, :, None, :]
    vim2 = vim * c1[None, :, None, :] - vre * s1[None, :, None, :]
    vst = jnp.concatenate([vre2, vim2], axis=1).reshape(2, 2 * g, r * by)
    uv = mm(fy3, vst, ((1,), (1,))).reshape(g, 2, r, by)
    back = lax.all_to_all(uv, "gy", 0, 0, tiled=True)
    return back, n


def rate_kernel(k_ref, w_ref, back_ref, bot_ref, side_ref, frc_ref, out_ref, ext_ref):
    rows, cols = ext_ref.shape[1], ext_ref.shape[2]
    bx, by = out_ref.shape
    g, _, r, _ = back_ref.shape

    ext_ref[0, :bx, :by] = w_ref[...]
    for f in range(2):
        for j in range(g):
            ext_ref[1 + f, j * r:(j + 1) * r, :by] = back_ref[j, f]
    for c in range(3):
        ext_ref[c, bx:, :] = bot_ref[c]
        ext_ref[c, :bx, by:] = side_ref[c]

    def rr(a, s):
        return pltpu.roll(a, s % rows, 0)

    def lr(a, s):
        return pltpu.roll(a, s % cols, 1)

    w = ext_ref[0]
    u = ext_ref[1]
    v = ext_ref[2]
    wm = rr(w, 1)
    wp = rr(w, -1)
    ym = lr(w, 1)
    yp = lr(w, -1)
    adv = (jnp.maximum(u, 0.0) * (w - wm) + jnp.minimum(u, 0.0) * (wp - w)
           + jnp.maximum(v, 0.0) * (w - ym) + jnp.minimum(v, 0.0) * (yp - w))
    lap = wp + wm + yp + ym - 4.0 * w
    gs = [None, None, None]
    for c, f in enumerate((w, u, v)):
        fm = wm if c == 0 else rr(f, 1)
        fp = wp if c == 0 else rr(f, -1)
        for b in range(3):
            term = (k_ref[9 * c + b] * fm + k_ref[9 * c + 3 + b] * f
                    + k_ref[9 * c + 6 + b] * fp)
            gs[b] = term if gs[b] is None else gs[b] + term
    clo = gs[1] + lr(gs[0], 1) + lr(gs[2], -1)
    res = -adv + VISCOSITY * lap - DRAG * w + clo
    out_ref[...] = res[:bx, :by] + frc_ref[0:1, :]


def halo(top, bottom, left, right):
    gx, gy = lax.axis_size("gx"), lax.axis_size("gy")

    def shift(x, axis, count, step):
        return lax.ppermute(x, axis, [(i, (i + step) % count) for i in range(count)])

    below = shift(top, "gx", gx, -1)
    above = shift(bottom, "gx", gx, 1)
    lcol = jnp.concatenate([above[:, :1], left, below[:, :1]], axis=1)
    rcol = jnp.concatenate([above[:, -1:], right, below[:, -1:]], axis=1)
    after = shift(lcol, "gy", gy, -1)
    before = shift(rcol, "gy", gy, 1)
    return (below, above, after[:, 1:-1], before[:, 1:-1],
            after[:, -1], before[:, -1], after[:, 0], before[:, 0])


def strips(parts, bx, by, rows, cols):
    below, above, after, before, c_br, c_bl, c_tr, c_tl = parts
    nc = below.shape[0]
    ri = jnp.arange(rows - bx, dtype=jnp.int32)[:, None]
    ci = jnp.arange(cols, dtype=jnp.int32)[None, :]
    pad = cols - by
    row_lo = jnp.concatenate([below, c_br[:, None], jnp.zeros((nc, pad - 2)), c_bl[:, None]], axis=1)
    row_hi = jnp.concatenate([above, c_tr[:, None], jnp.zeros((nc, pad - 2)), c_tl[:, None]], axis=1)
    bot = jnp.where(ri[None] == 0, row_lo[:, None, :],
                    jnp.where(ri[None] == rows - bx - 1, row_hi[:, None, :], 0.0))
    si = jnp.arange(pad, dtype=jnp.int32)[None, None, :]
    side = jnp.where(si == 0, after[:, :, None], jnp.where(si == pad - 1, before[:, :, None], 0.0))
    return bot, side


def per_device(vorticity, closure_kernel):
    bx, by = vorticity.shape
    rows = -(-(bx + 2) // 8) * 8
    cols = -(-(by + 2) // 128) * 128
    w = vorticity
    w_parts = halo(w[None, 0], w[None, -1], w[None, :, 0], w[None, :, -1])
    back, n = velocity(vorticity)
    uv_top = back[0, :, 0, :]
    uv_bot = back[-1, :, -1, :]
    uv_left = jnp.transpose(back[:, :, :, 0], (1, 0, 2)).reshape(2, bx)
    uv_right = jnp.transpose(back[:, :, :, -1], (1, 0, 2)).reshape(2, bx)
    uv_parts = halo(uv_top, uv_bot, uv_left, uv_right)
    parts = [jnp.concatenate([a, b], axis=0) for a, b in zip(w_parts, uv_parts)]
    bot, side = strips(parts, bx, by, rows, cols)
    columns = (lax.axis_index("gy") * by + jnp.arange(by, dtype=jnp.int32)).astype(jnp.float32)
    forcing = FORCE_AMP * jnp.cos(2.0 * math.pi * FORCE_WAVES / n * columns)
    frc = jnp.broadcast_to(forcing[None, :], (8, by))
    return pl.pallas_call(
        rate_kernel,
        out_shape=jax.ShapeDtypeStruct((bx, by), jnp.float32),
        in_specs=[pl.BlockSpec(memory_space=pltpu.SMEM)]
        + [pl.BlockSpec(memory_space=pltpu.VMEM)] * 5,
        out_specs=pl.BlockSpec(memory_space=pltpu.VMEM),
        scratch_shapes=[pltpu.VMEM((3, rows, cols), jnp.float32)],
        compiler_params=pltpu.CompilerParams(vmem_limit_bytes=60 * 1024 * 1024),
        cost_estimate=pl.CostEstimate(flops=60 * rows * cols, transcendentals=0,
                                      bytes_accessed=4 * (4 * rows * cols)),
    )(closure_kernel.reshape(-1), w, back, bot, side, frc)


def solution(mesh):
    placed = (P("gx", "gy"), P())
    return jax.shard_map(
        per_device, mesh=mesh, in_specs=placed, out_specs=P("gx", "gy"), check_vma=False
    )
```

```python
import math

import jax
import jax.numpy as jnp
from jax import lax
from jax.sharding import PartitionSpec as P
from jax.experimental import pallas as pl
from jax.experimental.pallas import tpu as pltpu

VISCOSITY = 0.5
DRAG = 0.1
FORCE_AMP = 1.0
FORCE_WAVES = 4.0
EXACT = lax.Precision.HIGH
BOTH = ("gx", "gy")


def mm(a, b, dims):
    return lax.dot_general(a, b, (dims, ((), ())), precision=EXACT,
                           preferred_element_type=jnp.float32)


def angle(rows, cols, period):
    idx = (jnp.arange(rows, dtype=jnp.int32)[:, None]
           * jnp.arange(cols, dtype=jnp.int32)[None, :]) % period
    return (2.0 * math.pi / period) * idx.astype(jnp.float32)


def velocity(w):
    g = lax.axis_size("gy")
    bx, by = w.shape
    n = by * g
    r = bx // g
    p = g * g
    k2n = n // 2 // g
    gr = g * r

    a16 = angle(g, g, g)
    fy1 = jnp.concatenate([jnp.cos(a16), -jnp.sin(a16)], axis=0)
    a1 = angle(g, by, n)
    c1, s1 = jnp.cos(a1), -jnp.sin(a1)
    a2 = angle(k2n, by, by)
    cy, sy = jnp.cos(a2), jnp.sin(a2)
    wre = jnp.concatenate([cy, sy], axis=1)
    wim = jnp.concatenate([-sy, cy], axis=1)
    ap = angle(p, p, p)
    fx1 = jnp.concatenate([jnp.cos(ap), jnp.sin(ap)], axis=0)
    at = angle(p, r, n)
    c2 = jnp.tile(jnp.cos(at), (1, g))
    s2 = jnp.tile(jnp.sin(at), (1, g))
    ar = angle(r, r, r)
    eye = jnp.eye(g, dtype=jnp.float32)
    ec = jnp.kron(eye, jnp.cos(ar))
    es = jnp.kron(eye, jnp.sin(ar))
    mfw = jnp.concatenate([jnp.concatenate([ec, -es], axis=1),
                           jnp.concatenate([es, ec], axis=1)], axis=0)
    mbw = jnp.concatenate([jnp.concatenate([ec, es], axis=1),
                           jnp.concatenate([-es, ec], axis=1)], axis=0)
    a3 = angle(g, g, g)
    fy3 = jnp.concatenate([jnp.cos(a3), -jnp.sin(a3)], axis=1)

    rows = lax.all_to_all(w.reshape(g, r, by), "gy", 0, 0, tiled=True)
    t = mm(fy1, rows.reshape(g, r * by), ((1,), (0,))).reshape(2, g, r, by)
    tre = t[0] * c1[:, None, :] - t[1] * s1[:, None, :]
    tim = t[0] * s1[:, None, :] + t[1] * c1[:, None, :]
    tcat = jnp.concatenate([tre, tim], axis=-1).reshape(gr, 2 * by)
    wr = mm(wre, tcat, ((1,), (1,)))
    wi = mm(wim, tcat, ((1,), (1,)))
    wcat = jnp.concatenate([wr, wi], axis=1)

    dx = lax.all_to_all(wcat, BOTH, 0, 0, tiled=True)
    z = mm(fx1, dx, ((1,), (0,)))
    z0, z1 = z[:p], z[p:]
    yre = z0[:, :gr] + z1[:, gr:]
    yim = z0[:, gr:] - z1[:, :gr]
    ycat = jnp.concatenate([yre * c2 + yim * s2, yim * c2 - yre * s2], axis=1)
    xh = mm(ycat, mfw, ((1,), (0,)))

    me = lax.axis_index("gx") * g + lax.axis_index("gy")
    col = jnp.arange(gr, dtype=jnp.int32)[None, :]
    k1x = jnp.arange(p, dtype=jnp.int32)[:, None]
    mx = k1x + p * (col % r)
    mx = jnp.where(mx < n // 2, mx, mx - n)
    ky_i = (col // r) % g + g * me
    kx = (2.0 * math.pi / n) * mx.astype(jnp.float32)
    ky = (2.0 * math.pi / n) * ky_i.astype(jnp.float32)
    sq = kx * kx + ky * ky
    pos = sq > 0.0
    inv = jnp.where(pos, 1.0 / jnp.where(pos, sq, 1.0), 0.0)
    weight = jnp.where(ky_i == 0, 1.0, 2.0) * (1.0 / (float(n) * float(n)))
    pre = xh[:, :gr] * inv
    pim = xh[:, gr:] * inv
    fu = ky * weight
    fv = kx * weight
    spec = jnp.concatenate([
        jnp.concatenate([-fu * pim, fu * pre], axis=1),
        jnp.concatenate([fv * pim, -fv * pre], axis=1),
    ], axis=0)

    q = mm(spec, mbw, ((1,), (0,)))
    qre, qim = q[:, :gr], q[:, gr:]
    c2b = jnp.concatenate([c2, c2], axis=0)
    s2b = jnp.concatenate([s2, s2], axis=0)
    qre2 = qre * c2b - qim * s2b
    qim2 = qre * s2b + qim * c2b
    qcat = jnp.concatenate([qre2[:p], qim2[:p], qre2[p:], qim2[p:]], axis=1)
    zb = mm(fx1, qcat, ((1,), (0,)))
    zb0, zb1 = zb[:p], zb[p:]
    parts = []
    for f in range(2):
        o = 2 * f * gr
        parts.append(zb0[:, o:o + gr] - zb1[:, o + gr:o + 2 * gr])
        parts.append(zb0[:, o + gr:o + 2 * gr] + zb1[:, o:o + gr])
    scat = jnp.concatenate(parts, axis=1)

    ey = lax.all_to_all(scat, BOTH, 0, 0, tiled=True)
    zz = mm(ey, wre, ((0,), (0,))).reshape(2, 2, g, r, 2 * by)
    vre = zz[:, 0, :, :, :by] - zz[:, 1, :, :, by:]
    vim = zz[:, 0, :, :, by:] + zz[:, 1, :, :, :by]
    vre2 = vre * c1[None, :, None, :] + vim * s1[None, :, None, :]
    vim2 = vim * c1[None, :, None, :] - vre * s1[None, :, None, :]
    vst = jnp.concatenate([vre2, vim2], axis=1).reshape(2, 2 * g, r * by)
    uv = mm(fy3, vst, ((1,), (1,))).reshape(g, 2, r, by)
    back = lax.all_to_all(uv, "gy", 0, 0, tiled=True)
    return back, n


def rate_kernel(k_ref, w_ref, back_ref, bot_ref, side_ref, frc_ref, out_ref, ext_ref):
    rows, cols = ext_ref.shape[1], ext_ref.shape[2]
    bx, by = out_ref.shape
    g, _, r, _ = back_ref.shape

    ext_ref[0, :bx, :by] = w_ref[...]
    for f in range(2):
        for j in range(g):
            ext_ref[1 + f, j * r:(j + 1) * r, :by] = back_ref[j, f]
    for c in range(3):
        ext_ref[c, bx:, :] = bot_ref[c]
        ext_ref[c, :bx, by:] = side_ref[c]

    def rr(a, s):
        return pltpu.roll(a, s % rows, 0)

    def lr(a, s):
        return pltpu.roll(a, s % cols, 1)

    w = ext_ref[0]
    u = ext_ref[1]
    v = ext_ref[2]
    wm = rr(w, 1)
    wp = rr(w, -1)
    ym = lr(w, 1)
    yp = lr(w, -1)
    adv = (jnp.maximum(u, 0.0) * (w - wm) + jnp.minimum(u, 0.0) * (wp - w)
           + jnp.maximum(v, 0.0) * (w - ym) + jnp.minimum(v, 0.0) * (yp - w))
    lap = wp + wm + yp + ym - 4.0 * w
    gs = [None, None, None]
    for c, f in enumerate((w, u, v)):
        fm = wm if c == 0 else rr(f, 1)
        fp = wp if c == 0 else rr(f, -1)
        for b in range(3):
            term = (k_ref[9 * c + b] * fm + k_ref[9 * c + 3 + b] * f
                    + k_ref[9 * c + 6 + b] * fp)
            gs[b] = term if gs[b] is None else gs[b] + term
    clo = gs[1] + lr(gs[0], 1) + lr(gs[2], -1)
    res = -adv + VISCOSITY * lap - DRAG * w + clo
    out_ref[...] = res[:bx, :by] + frc_ref[0:1, :]


def halo(top, bottom, left, right, corners):
    gx, gy = lax.axis_size("gx"), lax.axis_size("gy")

    def shift(x, axis, count, step):
        return lax.ppermute(x, axis, [(i, (i + step) % count) for i in range(count)])

    def diag(x, di, dj):
        pairs = []
        for i in range(gx):
            for j in range(gy):
                pairs.append((i * gy + j, ((i + di) % gx) * gy + (j + dj) % gy))
        return lax.ppermute(x, BOTH, pairs)

    below = shift(top, "gx", gx, -1)
    above = shift(bottom, "gx", gx, 1)
    after = shift(left, "gy", gy, -1)
    before = shift(right, "gy", gy, 1)
    c_br = diag(corners[:, 0], -1, -1)
    c_bl = diag(corners[:, 1], -1, 1)
    c_tr = diag(corners[:, 2], 1, -1)
    c_tl = diag(corners[:, 3], 1, 1)
    return below, above, after, before, c_br, c_bl, c_tr, c_tl


def strips(parts, bx, by, rows, cols):
    below, above, after, before, c_br, c_bl, c_tr, c_tl = parts
    nc = below.shape[0]
    ri = jnp.arange(rows - bx, dtype=jnp.int32)[:, None]
    ci = jnp.arange(cols, dtype=jnp.int32)[None, :]
    pad = cols - by
    row_lo = jnp.concatenate([below, c_br[:, None], jnp.zeros((nc, pad - 2)), c_bl[:, None]], axis=1)
    row_hi = jnp.concatenate([above, c_tr[:, None], jnp.zeros((nc, pad - 2)), c_tl[:, None]], axis=1)
    bot = jnp.where(ri[None] == 0, row_lo[:, None, :],
                    jnp.where(ri[None] == rows - bx - 1, row_hi[:, None, :], 0.0))
    si = jnp.arange(pad, dtype=jnp.int32)[None, None, :]
    side = jnp.where(si == 0, after[:, :, None], jnp.where(si == pad - 1, before[:, :, None], 0.0))
    return bot, side


def per_device(vorticity, closure_kernel):
    bx, by = vorticity.shape
    rows = -(-(bx + 2) // 8) * 8
    cols = -(-(by + 2) // 128) * 128
    w = vorticity
    w_parts = halo(w[None, 0], w[None, -1], w[None, :, 0], w[None, :, -1],
                   jnp.stack([w[0, 0], w[0, -1], w[-1, 0], w[-1, -1]])[None])
    back, n = velocity(vorticity)
    uv_top = back[0, :, 0, :]
    uv_bot = back[-1, :, -1, :]
    uv_left = jnp.transpose(back[:, :, :, 0], (1, 0, 2)).reshape(2, bx)
    uv_right = jnp.transpose(back[:, :, :, -1], (1, 0, 2)).reshape(2, bx)
    uv_corn = jnp.stack([uv_top[:, 0], uv_top[:, -1], uv_bot[:, 0], uv_bot[:, -1]], axis=1)
    uv_parts = halo(uv_top, uv_bot, uv_left, uv_right, uv_corn)
    parts = [jnp.concatenate([a, b], axis=0) for a, b in zip(w_parts, uv_parts)]
    bot, side = strips(parts, bx, by, rows, cols)
    columns = (lax.axis_index("gy") * by + jnp.arange(by, dtype=jnp.int32)).astype(jnp.float32)
    forcing = FORCE_AMP * jnp.cos(2.0 * math.pi * FORCE_WAVES / n * columns)
    frc = jnp.broadcast_to(forcing[None, :], (8, by))
    return pl.pallas_call(
        rate_kernel,
        out_shape=jax.ShapeDtypeStruct((bx, by), jnp.float32),
        in_specs=[pl.BlockSpec(memory_space=pltpu.SMEM)]
        + [pl.BlockSpec(memory_space=pltpu.VMEM)] * 5,
        out_specs=pl.BlockSpec(memory_space=pltpu.VMEM),
        scratch_shapes=[pltpu.VMEM((3, rows, cols), jnp.float32)],
        compiler_params=pltpu.CompilerParams(vmem_limit_bytes=60 * 1024 * 1024),
        cost_estimate=pl.CostEstimate(flops=60 * rows * cols, transcendentals=0,
                                      bytes_accessed=4 * (4 * rows * cols)),
    )(closure_kernel.reshape(-1), w, back, bot, side, frc)


def solution(mesh):
    placed = (P("gx", "gy"), P())
    return jax.shard_map(
        per_device, mesh=mesh, in_specs=placed, out_specs=P("gx", "gy"), check_vma=False
    )
```

```python
import math

import jax
import jax.numpy as jnp
from jax import lax
from jax.sharding import PartitionSpec as P
from jax.experimental import pallas as pl
from jax.experimental.pallas import tpu as pltpu

VISCOSITY = 0.5
DRAG = 0.1
FORCE_AMP = 1.0
FORCE_WAVES = 4.0
EXACT = lax.Precision.HIGHEST
BOTH = ("gx", "gy")


def mm(a, b, dims):
    return lax.dot_general(a, b, (dims, ((), ())), precision=EXACT,
                           preferred_element_type=jnp.float32)


def angle(rows, cols, period):
    idx = (jnp.arange(rows, dtype=jnp.int32)[:, None]
           * jnp.arange(cols, dtype=jnp.int32)[None, :]) % period
    return (2.0 * math.pi / period) * idx.astype(jnp.float32)


def velocity(w):
    g = lax.axis_size("gy")
    bx, by = w.shape
    n = by * g
    r = bx // g
    p = g * g
    k2n = n // 2 // g
    gr = g * r

    a16 = angle(g, g, g)
    fy1 = jnp.concatenate([jnp.cos(a16), -jnp.sin(a16)], axis=0)
    a1 = angle(g, by, n)
    c1, s1 = jnp.cos(a1), -jnp.sin(a1)
    a2 = angle(k2n, by, by)
    cy, sy = jnp.cos(a2), jnp.sin(a2)
    wre = jnp.concatenate([cy, sy], axis=1)
    wim = jnp.concatenate([-sy, cy], axis=1)
    ap = angle(p, p, p)
    fx1 = jnp.concatenate([jnp.cos(ap), jnp.sin(ap)], axis=0)
    at = angle(p, r, n)
    c2 = jnp.tile(jnp.cos(at), (1, g))
    s2 = jnp.tile(jnp.sin(at), (1, g))
    ar = angle(r, r, r)
    eye = jnp.eye(g, dtype=jnp.float32)
    ec = jnp.kron(eye, jnp.cos(ar))
    es = jnp.kron(eye, jnp.sin(ar))
    mfw = jnp.concatenate([jnp.concatenate([ec, -es], axis=1),
                           jnp.concatenate([es, ec], axis=1)], axis=0)
    mbw = jnp.concatenate([jnp.concatenate([ec, es], axis=1),
                           jnp.concatenate([-es, ec], axis=1)], axis=0)
    a3 = angle(g, g, g)
    fy3 = jnp.concatenate([jnp.cos(a3), -jnp.sin(a3)], axis=1)

    rows = lax.all_to_all(w.reshape(g, r, by), "gy", 0, 0, tiled=True)
    t = mm(fy1, rows.reshape(g, r * by), ((1,), (0,))).reshape(2, g, r, by)
    tre = t[0] * c1[:, None, :] - t[1] * s1[:, None, :]
    tim = t[0] * s1[:, None, :] + t[1] * c1[:, None, :]
    tcat = jnp.concatenate([tre, tim], axis=-1).reshape(gr, 2 * by)
    wr = mm(wre, tcat, ((1,), (1,)))
    wi = mm(wim, tcat, ((1,), (1,)))
    wcat = jnp.concatenate([wr, wi], axis=1)

    dx = lax.all_to_all(wcat.reshape(p, 8, -1), BOTH, 0, 0, tiled=True).reshape(p, 2 * gr)
    z = mm(fx1, dx, ((1,), (0,)))
    z0, z1 = z[:p], z[p:]
    yre = z0[:, :gr] + z1[:, gr:]
    yim = z0[:, gr:] - z1[:, :gr]
    ycat = jnp.concatenate([yre * c2 + yim * s2, yim * c2 - yre * s2], axis=1)
    xh = mm(ycat, mfw, ((1,), (0,)))

    me = lax.axis_index("gx") * g + lax.axis_index("gy")
    col = jnp.arange(gr, dtype=jnp.int32)[None, :]
    k1x = jnp.arange(p, dtype=jnp.int32)[:, None]
    mx = k1x + p * (col % r)
    mx = jnp.where(mx < n // 2, mx, mx - n)
    ky_i = (col // r) % g + g * me
    kx = (2.0 * math.pi / n) * mx.astype(jnp.float32)
    ky = (2.0 * math.pi / n) * ky_i.astype(jnp.float32)
    sq = kx * kx + ky * ky
    pos = sq > 0.0
    inv = jnp.where(pos, 1.0 / jnp.where(pos, sq, 1.0), 0.0)
    weight = jnp.where(ky_i == 0, 1.0, 2.0) * (1.0 / (float(n) * float(n)))
    pre = xh[:, :gr] * inv
    pim = xh[:, gr:] * inv
    fu = ky * weight
    fv = kx * weight
    spec = jnp.concatenate([
        jnp.concatenate([-fu * pim, fu * pre], axis=1),
        jnp.concatenate([fv * pim, -fv * pre], axis=1),
    ], axis=0)

    q = mm(spec, mbw, ((1,), (0,)))
    qre, qim = q[:, :gr], q[:, gr:]
    c2b = jnp.concatenate([c2, c2], axis=0)
    s2b = jnp.concatenate([s2, s2], axis=0)
    qre2 = qre * c2b - qim * s2b
    qim2 = qre * s2b + qim * c2b
    qcat = jnp.concatenate([qre2[:p], qim2[:p], qre2[p:], qim2[p:]], axis=1)
    zb = mm(fx1, qcat, ((1,), (0,)))
    zb0, zb1 = zb[:p], zb[p:]
    parts = []
    for f in range(2):
        o = 2 * f * gr
        parts.append(zb0[:, o:o + gr] - zb1[:, o + gr:o + 2 * gr])
        parts.append(zb0[:, o + gr:o + 2 * gr] + zb1[:, o:o + gr])
    scat = jnp.concatenate(parts, axis=1)

    ey = lax.all_to_all(scat.reshape(p, 8, -1), BOTH, 0, 0, tiled=True).reshape(p, 4 * gr)
    zz = mm(ey, wre, ((0,), (0,))).reshape(2, 2, g, r, 2 * by)
    vre = zz[:, 0, :, :, :by] - zz[:, 1, :, :, by:]
    vim = zz[:, 0, :, :, by:] + zz[:, 1, :, :, :by]
    vre2 = vre * c1[None, :, None, :] + vim * s1[None, :, None, :]
    vim2 = vim * c1[None, :, None, :] - vre * s1[None, :, None, :]
    vst = jnp.concatenate([vre2, vim2], axis=1).reshape(2, 2 * g, r * by)
    uv = mm(fy3, vst, ((1,), (1,))).reshape(g, 2, r, by)
    back = lax.all_to_all(uv, "gy", 0, 0, tiled=True)
    return back, n


def rate_kernel(k_ref, w_ref, back_ref, bot_ref, side_ref, frc_ref, out_ref, ext_ref):
    rows, cols = ext_ref.shape[1], ext_ref.shape[2]
    bx, by = out_ref.shape
    g, _, r, _ = back_ref.shape

    ext_ref[0, :bx, :by] = w_ref[...]
    for f in range(2):
        for j in range(g):
            ext_ref[1 + f, j * r:(j + 1) * r, :by] = back_ref[j, f]
    for c in range(3):
        ext_ref[c, bx:, :] = bot_ref[c]
        ext_ref[c, :bx, by:] = side_ref[c]

    def rr(a, s):
        return pltpu.roll(a, s % rows, 0)

    def lr(a, s):
        return pltpu.roll(a, s % cols, 1)

    w = ext_ref[0]
    u = ext_ref[1]
    v = ext_ref[2]
    wm = rr(w, 1)
    wp = rr(w, -1)
    ym = lr(w, 1)
    yp = lr(w, -1)
    adv = (jnp.maximum(u, 0.0) * (w - wm) + jnp.minimum(u, 0.0) * (wp - w)
           + jnp.maximum(v, 0.0) * (w - ym) + jnp.minimum(v, 0.0) * (yp - w))
    lap = wp + wm + yp + ym - 4.0 * w
    gs = [None, None, None]
    for c, f in enumerate((w, u, v)):
        fm = wm if c == 0 else rr(f, 1)
        fp = wp if c == 0 else rr(f, -1)
        for b in range(3):
            term = (k_ref[9 * c + b] * fm + k_ref[9 * c + 3 + b] * f
                    + k_ref[9 * c + 6 + b] * fp)
            gs[b] = term if gs[b] is None else gs[b] + term
    clo = gs[1] + lr(gs[0], 1) + lr(gs[2], -1)
    res = -adv + VISCOSITY * lap - DRAG * w + clo
    out_ref[...] = res[:bx, :by] + frc_ref[0:1, :]


def halo(top, bottom, left, right, corners):
    gx, gy = lax.axis_size("gx"), lax.axis_size("gy")

    def shift(x, axis, count, step):
        return lax.ppermute(x, axis, [(i, (i + step) % count) for i in range(count)])

    def diag(x, di, dj):
        pairs = []
        for i in range(gx):
            for j in range(gy):
                pairs.append((i * gy + j, ((i + di) % gx) * gy + (j + dj) % gy))
        return lax.ppermute(x, BOTH, pairs)

    below = shift(top, "gx", gx, -1)
    above = shift(bottom, "gx", gx, 1)
    after = shift(left, "gy", gy, -1)
    before = shift(right, "gy", gy, 1)
    c_br = diag(corners[:, 0], -1, -1)
    c_bl = diag(corners[:, 1], -1, 1)
    c_tr = diag(corners[:, 2], 1, -1)
    c_tl = diag(corners[:, 3], 1, 1)
    return below, above, after, before, c_br, c_bl, c_tr, c_tl


def strips(parts, bx, by, rows, cols):
    below, above, after, before, c_br, c_bl, c_tr, c_tl = parts
    nc = below.shape[0]
    ri = jnp.arange(rows - bx, dtype=jnp.int32)[:, None]
    ci = jnp.arange(cols, dtype=jnp.int32)[None, :]
    pad = cols - by
    row_lo = jnp.concatenate([below, c_br[:, None], jnp.zeros((nc, pad - 2)), c_bl[:, None]], axis=1)
    row_hi = jnp.concatenate([above, c_tr[:, None], jnp.zeros((nc, pad - 2)), c_tl[:, None]], axis=1)
    bot = jnp.where(ri[None] == 0, row_lo[:, None, :],
                    jnp.where(ri[None] == rows - bx - 1, row_hi[:, None, :], 0.0))
    si = jnp.arange(pad, dtype=jnp.int32)[None, None, :]
    side = jnp.where(si == 0, after[:, :, None], jnp.where(si == pad - 1, before[:, :, None], 0.0))
    return bot, side


def per_device(vorticity, closure_kernel):
    bx, by = vorticity.shape
    rows = -(-(bx + 2) // 8) * 8
    cols = -(-(by + 2) // 128) * 128
    w = vorticity
    w_parts = halo(w[None, 0], w[None, -1], w[None, :, 0], w[None, :, -1],
                   jnp.stack([w[0, 0], w[0, -1], w[-1, 0], w[-1, -1]])[None])
    back, n = velocity(vorticity)
    uv_top = back[0, :, 0, :]
    uv_bot = back[-1, :, -1, :]
    uv_left = jnp.transpose(back[:, :, :, 0], (1, 0, 2)).reshape(2, bx)
    uv_right = jnp.transpose(back[:, :, :, -1], (1, 0, 2)).reshape(2, bx)
    uv_corn = jnp.stack([uv_top[:, 0], uv_top[:, -1], uv_bot[:, 0], uv_bot[:, -1]], axis=1)
    uv_parts = halo(uv_top, uv_bot, uv_left, uv_right, uv_corn)
    parts = [jnp.concatenate([a, b], axis=0) for a, b in zip(w_parts, uv_parts)]
    bot, side = strips(parts, bx, by, rows, cols)
    columns = (lax.axis_index("gy") * by + jnp.arange(by, dtype=jnp.int32)).astype(jnp.float32)
    forcing = FORCE_AMP * jnp.cos(2.0 * math.pi * FORCE_WAVES / n * columns)
    frc = jnp.broadcast_to(forcing[None, :], (8, by))
    return pl.pallas_call(
        rate_kernel,
        out_shape=jax.ShapeDtypeStruct((bx, by), jnp.float32),
        in_specs=[pl.BlockSpec(memory_space=pltpu.SMEM)]
        + [pl.BlockSpec(memory_space=pltpu.VMEM)] * 5,
        out_specs=pl.BlockSpec(memory_space=pltpu.VMEM),
        scratch_shapes=[pltpu.VMEM((3, rows, cols), jnp.float32)],
        compiler_params=pltpu.CompilerParams(vmem_limit_bytes=60 * 1024 * 1024),
        cost_estimate=pl.CostEstimate(flops=60 * rows * cols, transcendentals=0,
                                      bytes_accessed=4 * (4 * rows * cols)),
    )(closure_kernel.reshape(-1), w, back, bot, side, frc)


def solution(mesh):
    placed = (P("gx", "gy"), P())
    return jax.shard_map(
        per_device, mesh=mesh, in_specs=placed, out_specs=P("gx", "gy"), check_vma=False
    )
```

```python
import math

import jax
import jax.numpy as jnp
from jax import lax
from jax.sharding import PartitionSpec as P
from jax.experimental import pallas as pl
from jax.experimental.pallas import tpu as pltpu

VISCOSITY = 0.5
DRAG = 0.1
FORCE_AMP = 1.0
FORCE_WAVES = 4.0
EXACT = lax.Precision.HIGHEST
BOTH = ("gx", "gy")


def mm(a, b, dims):
    return lax.dot_general(a, b, (dims, ((), ())), precision=EXACT,
                           preferred_element_type=jnp.float32)


def angle(rows, cols, period):
    idx = (jnp.arange(rows, dtype=jnp.int32)[:, None]
           * jnp.arange(cols, dtype=jnp.int32)[None, :]) % period
    return (2.0 * math.pi / period) * idx.astype(jnp.float32)


def velocity(w):
    g = lax.axis_size("gy")
    bx, by = w.shape
    n = by * g
    r = bx // g
    p = g * g
    k2n = n // 2 // g
    gr = g * r

    a16 = angle(g, g, g)
    fy1 = jnp.concatenate([jnp.cos(a16), -jnp.sin(a16)], axis=0)
    a1 = angle(g, by, n)
    c1, s1 = jnp.cos(a1), -jnp.sin(a1)
    a2 = angle(k2n, by, by)
    cy, sy = jnp.cos(a2), jnp.sin(a2)
    wre = jnp.concatenate([cy, sy], axis=1)
    wim = jnp.concatenate([-sy, cy], axis=1)
    ap = angle(p, p, p)
    fx1 = jnp.concatenate([jnp.cos(ap), jnp.sin(ap)], axis=0)
    at = angle(p, r, n)
    c2 = jnp.tile(jnp.cos(at), (1, g))
    s2 = jnp.tile(jnp.sin(at), (1, g))
    ar = angle(r, r, r)
    eye = jnp.eye(g, dtype=jnp.float32)
    ec = jnp.kron(eye, jnp.cos(ar))
    es = jnp.kron(eye, jnp.sin(ar))
    mfw = jnp.concatenate([jnp.concatenate([ec, -es], axis=1),
                           jnp.concatenate([es, ec], axis=1)], axis=0)
    mbw = jnp.concatenate([jnp.concatenate([ec, es], axis=1),
                           jnp.concatenate([-es, ec], axis=1)], axis=0)
    a3 = angle(g, g, g)
    fy3 = jnp.concatenate([jnp.cos(a3), -jnp.sin(a3)], axis=1)

    rows = lax.all_to_all(w.reshape(g, r, by), "gy", 0, 0, tiled=True)
    t = mm(fy1, rows.reshape(g, r * by), ((1,), (0,))).reshape(2, g, r, by)
    tre = t[0] * c1[:, None, :] - t[1] * s1[:, None, :]
    tim = t[0] * s1[:, None, :] + t[1] * c1[:, None, :]
    tcat = jnp.concatenate([tre, tim], axis=-1).reshape(gr, 2 * by)
    wr = mm(wre, tcat, ((1,), (1,)))
    wi = mm(wim, tcat, ((1,), (1,)))
    wcat = jnp.concatenate([wr, wi], axis=1)

    dx = lax.all_to_all(wcat, BOTH, 0, 0, tiled=True)
    z = mm(fx1, dx, ((1,), (0,)))
    z0, z1 = z[:p], z[p:]
    yre = z0[:, :gr] + z1[:, gr:]
    yim = z0[:, gr:] - z1[:, :gr]
    ycat = jnp.concatenate([yre * c2 + yim * s2, yim * c2 - yre * s2], axis=1)
    xh = mm(ycat, mfw, ((1,), (0,)))

    me = lax.axis_index("gx") * g + lax.axis_index("gy")
    col = jnp.arange(gr, dtype=jnp.int32)[None, :]
    k1x = jnp.arange(p, dtype=jnp.int32)[:, None]
    mx = k1x + p * (col % r)
    mx = jnp.where(mx < n // 2, mx, mx - n)
    ky_i = (col // r) % g + g * me
    kx = (2.0 * math.pi / n) * mx.astype(jnp.float32)
    ky = (2.0 * math.pi / n) * ky_i.astype(jnp.float32)
    sq = kx * kx + ky * ky
    pos = sq > 0.0
    inv = jnp.where(pos, 1.0 / jnp.where(pos, sq, 1.0), 0.0)
    weight = jnp.where(ky_i == 0, 1.0, 2.0) * (1.0 / (float(n) * float(n)))
    pre = xh[:, :gr] * inv
    pim = xh[:, gr:] * inv
    fu = ky * weight
    fv = kx * weight
    spec = jnp.concatenate([
        jnp.concatenate([-fu * pim, fu * pre], axis=1),
        jnp.concatenate([fv * pim, -fv * pre], axis=1),
    ], axis=0)

    q = mm(spec, mbw, ((1,), (0,)))
    qre, qim = q[:, :gr], q[:, gr:]
    c2b = jnp.concatenate([c2, c2], axis=0)
    s2b = jnp.concatenate([s2, s2], axis=0)
    qre2 = qre * c2b - qim * s2b
    qim2 = qre * s2b + qim * c2b
    qcat = jnp.concatenate([qre2[:p], qim2[:p], qre2[p:], qim2[p:]], axis=1)
    zb = mm(fx1, qcat, ((1,), (0,)))
    zb0, zb1 = zb[:p], zb[p:]
    parts = []
    for f in range(2):
        o = 2 * f * gr
        parts.append(zb0[:, o:o + gr] - zb1[:, o + gr:o + 2 * gr])
        parts.append(zb0[:, o + gr:o + 2 * gr] + zb1[:, o:o + gr])
    scat = jnp.concatenate(parts, axis=1)

    ey = lax.all_to_all(scat, BOTH, 0, 0, tiled=True)
    zz = mm(ey, wre, ((0,), (0,))).reshape(2, 2, g, r, 2 * by)
    vre = zz[:, 0, :, :, :by] - zz[:, 1, :, :, by:]
    vim = zz[:, 0, :, :, by:] + zz[:, 1, :, :, :by]
    vre2 = vre * c1[None, :, None, :] + vim * s1[None, :, None, :]
    vim2 = vim * c1[None, :, None, :] - vre * s1[None, :, None, :]
    vst = jnp.concatenate([vre2, vim2], axis=1).reshape(2, 2 * g, r * by)
    uv = mm(fy3, vst, ((1,), (1,))).reshape(g, 2, r, by)
    back = lax.all_to_all(uv, "gy", 0, 0, tiled=True)
    sides = jnp.stack([jnp.roll(uv[:, :, :, -1], 1, axis=0),
                       jnp.roll(uv[:, :, :, 0], -1, axis=0)], axis=-1).reshape(g, 4 * r)
    sides = lax.all_to_all(sides, "gy", 0, 0, tiled=True).reshape(g, 2, r, 2)
    before = jnp.transpose(sides[..., 0], (1, 0, 2)).reshape(2, bx)
    after = jnp.transpose(sides[..., 1], (1, 0, 2)).reshape(2, bx)
    return back, before, after, n


def rate_kernel(k_ref, w_ref, back_ref, bot_ref, side_ref, frc_ref, out_ref, ext_ref):
    rows, cols = ext_ref.shape[1], ext_ref.shape[2]
    bx, by = out_ref.shape
    g, _, r, _ = back_ref.shape

    ext_ref[0, :bx, :by] = w_ref[...]
    for f in range(2):
        for j in range(g):
            ext_ref[1 + f, j * r:(j + 1) * r, :by] = back_ref[j, f]
    for c in range(3):
        ext_ref[c, bx:, :] = bot_ref[c]
        ext_ref[c, :bx, by:] = side_ref[c]

    def rr(a, s):
        return pltpu.roll(a, s % rows, 0)

    def lr(a, s):
        return pltpu.roll(a, s % cols, 1)

    w = ext_ref[0]
    u = ext_ref[1]
    v = ext_ref[2]
    wm = rr(w, 1)
    wp = rr(w, -1)
    ym = lr(w, 1)
    yp = lr(w, -1)
    adv = (jnp.maximum(u, 0.0) * (w - wm) + jnp.minimum(u, 0.0) * (wp - w)
           + jnp.maximum(v, 0.0) * (w - ym) + jnp.minimum(v, 0.0) * (yp - w))
    lap = wp + wm + yp + ym - 4.0 * w
    gs = [None, None, None]
    for c, f in enumerate((w, u, v)):
        fm = wm if c == 0 else rr(f, 1)
        fp = wp if c == 0 else rr(f, -1)
        for b in range(3):
            term = (k_ref[9 * c + b] * fm + k_ref[9 * c + 3 + b] * f
                    + k_ref[9 * c + 6 + b] * fp)
            gs[b] = term if gs[b] is None else gs[b] + term
    clo = gs[1] + lr(gs[0], 1) + lr(gs[2], -1)
    res = -adv + VISCOSITY * lap - DRAG * w + clo
    out_ref[...] = res[:bx, :by] + frc_ref[0:1, :]


def halo(top, bottom, left, right, corners):
    gx, gy = lax.axis_size("gx"), lax.axis_size("gy")

    def shift(x, axis, count, step):
        return lax.ppermute(x, axis, [(i, (i + step) % count) for i in range(count)])

    def diag(x, di, dj):
        pairs = []
        for i in range(gx):
            for j in range(gy):
                pairs.append((i * gy + j, ((i + di) % gx) * gy + (j + dj) % gy))
        return lax.ppermute(x, BOTH, pairs)

    below = shift(top, "gx", gx, -1)
    above = shift(bottom, "gx", gx, 1)
    after = shift(left, "gy", gy, -1)
    before = shift(right, "gy", gy, 1)
    c_br = diag(corners[:, 0], -1, -1)
    c_bl = diag(corners[:, 1], -1, 1)
    c_tr = diag(corners[:, 2], 1, -1)
    c_tl = diag(corners[:, 3], 1, 1)
    return below, above, after, before, c_br, c_bl, c_tr, c_tl


def strips(parts, bx, by, rows, cols):
    below, above, after, before, c_br, c_bl, c_tr, c_tl = parts
    nc = below.shape[0]
    ri = jnp.arange(rows - bx, dtype=jnp.int32)[:, None]
    ci = jnp.arange(cols, dtype=jnp.int32)[None, :]
    pad = cols - by
    row_lo = jnp.concatenate([below, c_br[:, None], jnp.zeros((nc, pad - 2)), c_bl[:, None]], axis=1)
    row_hi = jnp.concatenate([above, c_tr[:, None], jnp.zeros((nc, pad - 2)), c_tl[:, None]], axis=1)
    bot = jnp.where(ri[None] == 0, row_lo[:, None, :],
                    jnp.where(ri[None] == rows - bx - 1, row_hi[:, None, :], 0.0))
    si = jnp.arange(pad, dtype=jnp.int32)[None, None, :]
    side = jnp.where(si == 0, after[:, :, None], jnp.where(si == pad - 1, before[:, :, None], 0.0))
    return bot, side


def per_device(vorticity, closure_kernel):
    bx, by = vorticity.shape
    rows = -(-(bx + 2) // 8) * 8
    cols = -(-(by + 2) // 128) * 128
    w = vorticity
    w_parts = halo(w[None, 0], w[None, -1], w[None, :, 0], w[None, :, -1],
                   jnp.stack([w[0, 0], w[0, -1], w[-1, 0], w[-1, -1]])[None])
    back, before, after, n = velocity(vorticity)
    gx = lax.axis_size("gx")
    top = jnp.concatenate([before[:, :1], back[0, :, 0, :], after[:, :1]], axis=1)
    bottom = jnp.concatenate([before[:, -1:], back[-1, :, -1, :], after[:, -1:]], axis=1)
    below = lax.ppermute(top, "gx", [(i, (i - 1) % gx) for i in range(gx)])
    above = lax.ppermute(bottom, "gx", [(i, (i + 1) % gx) for i in range(gx)])
    uv_parts = (below[:, 1:-1], above[:, 1:-1], after, before,
                below[:, -1], below[:, 0], above[:, -1], above[:, 0])
    parts = [jnp.concatenate([a, b], axis=0) for a, b in zip(w_parts, uv_parts)]
    bot, side = strips(parts, bx, by, rows, cols)
    columns = (lax.axis_index("gy") * by + jnp.arange(by, dtype=jnp.int32)).astype(jnp.float32)
    forcing = FORCE_AMP * jnp.cos(2.0 * math.pi * FORCE_WAVES / n * columns)
    frc = jnp.broadcast_to(forcing[None, :], (8, by))
    return pl.pallas_call(
        rate_kernel,
        out_shape=jax.ShapeDtypeStruct((bx, by), jnp.float32),
        in_specs=[pl.BlockSpec(memory_space=pltpu.SMEM)]
        + [pl.BlockSpec(memory_space=pltpu.VMEM)] * 5,
        out_specs=pl.BlockSpec(memory_space=pltpu.VMEM),
        scratch_shapes=[pltpu.VMEM((3, rows, cols), jnp.float32)],
        compiler_params=pltpu.CompilerParams(vmem_limit_bytes=60 * 1024 * 1024),
        cost_estimate=pl.CostEstimate(flops=60 * rows * cols, transcendentals=0,
                                      bytes_accessed=4 * (4 * rows * cols)),
    )(closure_kernel.reshape(-1), w, back, bot, side, frc)


def solution(mesh):
    placed = (P("gx", "gy"), P())
    return jax.shard_map(
        per_device, mesh=mesh, in_specs=placed, out_specs=P("gx", "gy"), check_vma=False
    )
```

```python
import math

import jax
import jax.numpy as jnp
from jax import lax
from jax.sharding import PartitionSpec as P
from jax.experimental import pallas as pl
from jax.experimental.pallas import tpu as pltpu

VISCOSITY = 0.5
DRAG = 0.1
FORCE_AMP = 1.0
FORCE_WAVES = 4.0
EXACT = lax.Precision.HIGHEST
BOTH = ("gx", "gy")


def mm(a, b, dims):
    return lax.dot_general(a, b, (dims, ((), ())), precision=EXACT,
                           preferred_element_type=jnp.float32)


def angle(rows, cols, period):
    idx = (jnp.arange(rows, dtype=jnp.int32)[:, None]
           * jnp.arange(cols, dtype=jnp.int32)[None, :]) % period
    return (2.0 * math.pi / period) * idx.astype(jnp.float32)


def velocity(w):
    g = lax.axis_size("gy")
    bx, by = w.shape
    n = by * g
    r = bx // g
    p = g * g
    k2n = n // 2 // g
    gr = g * r

    a16 = angle(g, g, g)
    fy1 = jnp.concatenate([jnp.cos(a16), -jnp.sin(a16)], axis=0)
    a1 = angle(g, by, n)
    c1, s1 = jnp.cos(a1), -jnp.sin(a1)
    a2 = angle(k2n, by, by)
    cy, sy = jnp.cos(a2), jnp.sin(a2)
    wre = jnp.concatenate([cy, sy], axis=1)
    wim = jnp.concatenate([-sy, cy], axis=1)
    ap = angle(p, p, p)
    fx1 = jnp.concatenate([jnp.cos(ap), jnp.sin(ap)], axis=0)
    at = angle(p, r, n)
    c2 = jnp.tile(jnp.cos(at), (1, g))
    s2 = jnp.tile(jnp.sin(at), (1, g))
    ar = angle(r, r, r)
    eye = jnp.eye(g, dtype=jnp.float32)
    ec = jnp.kron(eye, jnp.cos(ar))
    es = jnp.kron(eye, jnp.sin(ar))
    mfw = jnp.concatenate([jnp.concatenate([ec, -es], axis=1),
                           jnp.concatenate([es, ec], axis=1)], axis=0)
    mbw = jnp.concatenate([jnp.concatenate([ec, es], axis=1),
                           jnp.concatenate([-es, ec], axis=1)], axis=0)
    a3 = angle(g, g, g)
    fy3 = jnp.concatenate([jnp.cos(a3), -jnp.sin(a3)], axis=1)

    rows = lax.all_to_all(w.reshape(g, r, by), "gy", 0, 0, tiled=True)
    t = mm(fy1, rows.reshape(g, r * by), ((1,), (0,))).reshape(2, g, r, by)
    tre = t[0] * c1[:, None, :] - t[1] * s1[:, None, :]
    tim = t[0] * s1[:, None, :] + t[1] * c1[:, None, :]
    tcat = jnp.concatenate([tre, tim], axis=-1).reshape(gr, 2 * by)
    wr = mm(wre, tcat, ((1,), (1,)))
    wi = mm(wim, tcat, ((1,), (1,)))
    wcat = jnp.concatenate([wr, wi], axis=1)

    dx = lax.all_to_all(wcat, BOTH, 0, 0, tiled=True)
    z = mm(fx1, dx, ((1,), (0,)))
    z0, z1 = z[:p], z[p:]
    yre = z0[:, :gr] + z1[:, gr:]
    yim = z0[:, gr:] - z1[:, :gr]
    ycat = jnp.concatenate([yre * c2 + yim * s2, yim * c2 - yre * s2], axis=1)
    xh = mm(ycat, mfw, ((1,), (0,)))

    me = lax.axis_index("gx") * g + lax.axis_index("gy")
    col = jnp.arange(gr, dtype=jnp.int32)[None, :]
    k1x = jnp.arange(p, dtype=jnp.int32)[:, None]
    mx = k1x + p * (col % r)
    mx = jnp.where(mx < n // 2, mx, mx - n)
    ky_i = (col // r) % g + g * me
    kx = (2.0 * math.pi / n) * mx.astype(jnp.float32)
    ky = (2.0 * math.pi / n) * ky_i.astype(jnp.float32)
    sq = kx * kx + ky * ky
    pos = sq > 0.0
    inv = jnp.where(pos, 1.0 / jnp.where(pos, sq, 1.0), 0.0)
    weight = jnp.where(ky_i == 0, 1.0, 2.0) * (1.0 / (float(n) * float(n)))
    pre = xh[:, :gr] * inv
    pim = xh[:, gr:] * inv
    fu = ky * weight
    fv = kx * weight
    spec = jnp.concatenate([
        jnp.concatenate([-fu * pim, fu * pre], axis=1),
        jnp.concatenate([fv * pim, -fv * pre], axis=1),
    ], axis=0)

    q = mm(spec, mbw, ((1,), (0,)))
    qre, qim = q[:, :gr], q[:, gr:]
    c2b = jnp.concatenate([c2, c2], axis=0)
    s2b = jnp.concatenate([s2, s2], axis=0)
    qre2 = qre * c2b - qim * s2b
    qim2 = qre * s2b + qim * c2b
    qcat = jnp.concatenate([qre2[:p], qim2[:p], qre2[p:], qim2[p:]], axis=1)
    zb = mm(fx1, qcat, ((1,), (0,)))
    zb0, zb1 = zb[:p], zb[p:]
    parts = []
    for f in range(2):
        o = 2 * f * gr
        parts.append(zb0[:, o:o + gr] - zb1[:, o + gr:o + 2 * gr])
        parts.append(zb0[:, o + gr:o + 2 * gr] + zb1[:, o:o + gr])
    scat = jnp.concatenate(parts, axis=1)

    ey = lax.all_to_all(scat, BOTH, 0, 0, tiled=True)
    zz = mm(ey, wre, ((0,), (0,))).reshape(2, 2, g, r, 2 * by)
    vre = zz[:, 0, :, :, :by] - zz[:, 1, :, :, by:]
    vim = zz[:, 0, :, :, by:] + zz[:, 1, :, :, :by]
    vre2 = vre * c1[None, :, None, :] + vim * s1[None, :, None, :]
    vim2 = vim * c1[None, :, None, :] - vre * s1[None, :, None, :]
    vst = jnp.concatenate([vre2, vim2], axis=1).reshape(2, 2 * g, r * by)
    uv = mm(fy3, vst, ((1,), (1,))).reshape(g, 2, r, by)
    sides = jnp.stack([jnp.roll(uv[:, :, :, -1], 1, axis=0),
                       jnp.roll(uv[:, :, :, 0], -1, axis=0)], axis=-1).reshape(g, 1, 4 * r)
    slab = jnp.pad(sides, ((0, 0), (0, 7), (0, by - 4 * r)))
    payload = jnp.concatenate([uv.reshape(g, 2 * r, by), slab], axis=1)
    back = lax.all_to_all(payload, "gy", 0, 0, tiled=True)
    sides = back[:, 2 * r, :4 * r].reshape(g, 2, r, 2)
    before = jnp.transpose(sides[..., 0], (1, 0, 2)).reshape(2, bx)
    after = jnp.transpose(sides[..., 1], (1, 0, 2)).reshape(2, bx)
    return back, before, after, n


def rate_kernel(k_ref, w_ref, back_ref, bot_ref, side_ref, frc_ref, out_ref, ext_ref):
    rows, cols = ext_ref.shape[1], ext_ref.shape[2]
    bx, by = out_ref.shape
    g = back_ref.shape[0]
    r = bx // g

    ext_ref[0, :bx, :by] = w_ref[...]
    for f in range(2):
        for j in range(g):
            ext_ref[1 + f, j * r:(j + 1) * r, :by] = back_ref[j, f * r:(f + 1) * r]
    for c in range(3):
        ext_ref[c, bx:, :] = bot_ref[c]
        ext_ref[c, :bx, by:] = side_ref[c]

    def rr(a, s):
        return pltpu.roll(a, s % rows, 0)

    def lr(a, s):
        return pltpu.roll(a, s % cols, 1)

    w = ext_ref[0]
    u = ext_ref[1]
    v = ext_ref[2]
    wm = rr(w, 1)
    wp = rr(w, -1)
    ym = lr(w, 1)
    yp = lr(w, -1)
    adv = (jnp.maximum(u, 0.0) * (w - wm) + jnp.minimum(u, 0.0) * (wp - w)
           + jnp.maximum(v, 0.0) * (w - ym) + jnp.minimum(v, 0.0) * (yp - w))
    lap = wp + wm + yp + ym - 4.0 * w
    gs = [None, None, None]
    for c, f in enumerate((w, u, v)):
        fm = wm if c == 0 else rr(f, 1)
        fp = wp if c == 0 else rr(f, -1)
        for b in range(3):
            term = (k_ref[9 * c + b] * fm + k_ref[9 * c + 3 + b] * f
                    + k_ref[9 * c + 6 + b] * fp)
            gs[b] = term if gs[b] is None else gs[b] + term
    clo = gs[1] + lr(gs[0], 1) + lr(gs[2], -1)
    res = -adv + VISCOSITY * lap - DRAG * w + clo
    out_ref[...] = res[:bx, :by] + frc_ref[0:1, :]


def halo(top, bottom, left, right, corners):
    gx, gy = lax.axis_size("gx"), lax.axis_size("gy")

    def shift(x, axis, count, step):
        return lax.ppermute(x, axis, [(i, (i + step) % count) for i in range(count)])

    def diag(x, di, dj):
        pairs = []
        for i in range(gx):
            for j in range(gy):
                pairs.append((i * gy + j, ((i + di) % gx) * gy + (j + dj) % gy))
        return lax.ppermute(x, BOTH, pairs)

    below = shift(top, "gx", gx, -1)
    above = shift(bottom, "gx", gx, 1)
    after = shift(left, "gy", gy, -1)
    before = shift(right, "gy", gy, 1)
    c_br = diag(corners[:, 0], -1, -1)
    c_bl = diag(corners[:, 1], -1, 1)
    c_tr = diag(corners[:, 2], 1, -1)
    c_tl = diag(corners[:, 3], 1, 1)
    return below, above, after, before, c_br, c_bl, c_tr, c_tl


def strips(parts, bx, by, rows, cols):
    below, above, after, before, c_br, c_bl, c_tr, c_tl = parts
    nc = below.shape[0]
    ri = jnp.arange(rows - bx, dtype=jnp.int32)[:, None]
    ci = jnp.arange(cols, dtype=jnp.int32)[None, :]
    pad = cols - by
    row_lo = jnp.concatenate([below, c_br[:, None], jnp.zeros((nc, pad - 2)), c_bl[:, None]], axis=1)
    row_hi = jnp.concatenate([above, c_tr[:, None], jnp.zeros((nc, pad - 2)), c_tl[:, None]], axis=1)
    bot = jnp.where(ri[None] == 0, row_lo[:, None, :],
                    jnp.where(ri[None] == rows - bx - 1, row_hi[:, None, :], 0.0))
    si = jnp.arange(pad, dtype=jnp.int32)[None, None, :]
    side = jnp.where(si == 0, after[:, :, None], jnp.where(si == pad - 1, before[:, :, None], 0.0))
    return bot, side


def per_device(vorticity, closure_kernel):
    bx, by = vorticity.shape
    rows = -(-(bx + 2) // 8) * 8
    cols = -(-(by + 2) // 128) * 128
    w = vorticity
    w_parts = halo(w[None, 0], w[None, -1], w[None, :, 0], w[None, :, -1],
                   jnp.stack([w[0, 0], w[0, -1], w[-1, 0], w[-1, -1]])[None])
    back, before, after, n = velocity(vorticity)
    gx = lax.axis_size("gx")
    r = bx // back.shape[0]
    top = jnp.concatenate([before[:, :1], back[0, 0:2 * r:r, :], after[:, :1]], axis=1)
    bottom = jnp.concatenate([before[:, -1:], back[-1, r - 1:2 * r:r, :], after[:, -1:]], axis=1)
    below = lax.ppermute(top, "gx", [(i, (i - 1) % gx) for i in range(gx)])
    above = lax.ppermute(bottom, "gx", [(i, (i + 1) % gx) for i in range(gx)])
    uv_parts = (below[:, 1:-1], above[:, 1:-1], after, before,
                below[:, -1], below[:, 0], above[:, -1], above[:, 0])
    parts = [jnp.concatenate([a, b], axis=0) for a, b in zip(w_parts, uv_parts)]
    bot, side = strips(parts, bx, by, rows, cols)
    columns = (lax.axis_index("gy") * by + jnp.arange(by, dtype=jnp.int32)).astype(jnp.float32)
    forcing = FORCE_AMP * jnp.cos(2.0 * math.pi * FORCE_WAVES / n * columns)
    frc = jnp.broadcast_to(forcing[None, :], (8, by))
    return pl.pallas_call(
        rate_kernel,
        out_shape=jax.ShapeDtypeStruct((bx, by), jnp.float32),
        in_specs=[pl.BlockSpec(memory_space=pltpu.SMEM)]
        + [pl.BlockSpec(memory_space=pltpu.VMEM)] * 5,
        out_specs=pl.BlockSpec(memory_space=pltpu.VMEM),
        scratch_shapes=[pltpu.VMEM((3, rows, cols), jnp.float32)],
        compiler_params=pltpu.CompilerParams(vmem_limit_bytes=60 * 1024 * 1024),
        cost_estimate=pl.CostEstimate(flops=60 * rows * cols, transcendentals=0,
                                      bytes_accessed=4 * (4 * rows * cols)),
    )(closure_kernel.reshape(-1), w, back, bot, side, frc)


def solution(mesh):
    placed = (P("gx", "gy"), P())
    return jax.shard_map(
        per_device, mesh=mesh, in_specs=placed, out_specs=P("gx", "gy"), check_vma=False
    )
```

```python
import math

import jax
import jax.numpy as jnp
from jax import lax
from jax.sharding import PartitionSpec as P
from jax.experimental import pallas as pl
from jax.experimental.pallas import tpu as pltpu

VISCOSITY = 0.5
DRAG = 0.1
FORCE_AMP = 1.0
FORCE_WAVES = 4.0
EXACT = lax.Precision.HIGHEST
BOTH = ("gx", "gy")


def mm(a, b, dims):
    return lax.dot_general(a, b, (dims, ((), ())), precision=EXACT,
                           preferred_element_type=jnp.float32)


def angle(rows, cols, period):
    idx = (jnp.arange(rows, dtype=jnp.int32)[:, None]
           * jnp.arange(cols, dtype=jnp.int32)[None, :]) % period
    return (2.0 * math.pi / period) * idx.astype(jnp.float32)


def velocity(w):
    g = lax.axis_size("gy")
    bx, by = w.shape
    n = by * g
    r = bx // g
    p = g * g
    k2n = n // 2 // g
    gr = g * r

    a16 = angle(g, g, g)
    fy1 = jnp.concatenate([jnp.cos(a16), -jnp.sin(a16)], axis=0)
    a1 = angle(g, by, n)
    c1, s1 = jnp.cos(a1), -jnp.sin(a1)
    a2 = angle(k2n, by, by)
    cy, sy = jnp.cos(a2), jnp.sin(a2)
    wre = jnp.concatenate([cy, sy], axis=1)
    wim = jnp.concatenate([-sy, cy], axis=1)
    ap = angle(p, p, p)
    fx1 = jnp.concatenate([jnp.cos(ap), jnp.sin(ap)], axis=0)
    at = angle(p, r, n)
    c2 = jnp.tile(jnp.cos(at), (1, g))
    s2 = jnp.tile(jnp.sin(at), (1, g))
    ar = angle(r, r, r)
    eye = jnp.eye(g, dtype=jnp.float32)
    ec = jnp.kron(eye, jnp.cos(ar))
    es = jnp.kron(eye, jnp.sin(ar))
    mfw = jnp.concatenate([jnp.concatenate([ec, -es], axis=1),
                           jnp.concatenate([es, ec], axis=1)], axis=0)
    mbw = jnp.concatenate([jnp.concatenate([ec, es], axis=1),
                           jnp.concatenate([-es, ec], axis=1)], axis=0)
    a3 = angle(g, g, g)
    fy3 = jnp.concatenate([jnp.cos(a3), -jnp.sin(a3)], axis=1)

    rows = lax.all_to_all(w.reshape(g, r, by), "gy", 0, 0, tiled=True)
    t = mm(fy1, rows.reshape(g, r * by), ((1,), (0,))).reshape(2, g, r, by)
    tre = t[0] * c1[:, None, :] - t[1] * s1[:, None, :]
    tim = t[0] * s1[:, None, :] + t[1] * c1[:, None, :]
    tcat = jnp.concatenate([tre, tim], axis=-1).reshape(gr, 2 * by)
    wr = mm(wre, tcat, ((1,), (1,)))
    wi = mm(wim, tcat, ((1,), (1,)))
    wcat = jnp.concatenate([wr, wi], axis=1)

    dx = lax.all_to_all(wcat, BOTH, 0, 0, tiled=True)
    z = mm(fx1, dx, ((1,), (0,)))
    z0, z1 = z[:p], z[p:]
    yre = z0[:, :gr] + z1[:, gr:]
    yim = z0[:, gr:] - z1[:, :gr]
    ycat = jnp.concatenate([yre * c2 + yim * s2, yim * c2 - yre * s2], axis=1)
    xh = mm(ycat, mfw, ((1,), (0,)))

    me = lax.axis_index("gx") * g + lax.axis_index("gy")
    col = jnp.arange(gr, dtype=jnp.int32)[None, :]
    k1x = jnp.arange(p, dtype=jnp.int32)[:, None]
    mx = k1x + p * (col % r)
    mx = jnp.where(mx < n // 2, mx, mx - n)
    ky_i = (col // r) % g + g * me
    kx = (2.0 * math.pi / n) * mx.astype(jnp.float32)
    ky = (2.0 * math.pi / n) * ky_i.astype(jnp.float32)
    sq = kx * kx + ky * ky
    pos = sq > 0.0
    inv = jnp.where(pos, 1.0 / jnp.where(pos, sq, 1.0), 0.0)
    weight = jnp.where(ky_i == 0, 1.0, 2.0) * (1.0 / (float(n) * float(n)))
    pre = xh[:, :gr] * inv
    pim = xh[:, gr:] * inv
    fu = ky * weight
    fv = kx * weight
    spec = jnp.concatenate([
        jnp.concatenate([-fu * pim, fu * pre], axis=1),
        jnp.concatenate([fv * pim, -fv * pre], axis=1),
    ], axis=0)

    q = mm(spec, mbw, ((1,), (0,)))
    qre, qim = q[:, :gr], q[:, gr:]
    c2b = jnp.concatenate([c2, c2], axis=0)
    s2b = jnp.concatenate([s2, s2], axis=0)
    qre2 = qre * c2b - qim * s2b
    qim2 = qre * s2b + qim * c2b
    qcat = jnp.concatenate([qre2[:p], qim2[:p], qre2[p:], qim2[p:]], axis=1)
    zb = mm(fx1, qcat, ((1,), (0,)))
    zb0, zb1 = zb[:p], zb[p:]
    parts = []
    for f in range(2):
        o = 2 * f * gr
        parts.append(zb0[:, o:o + gr] - zb1[:, o + gr:o + 2 * gr])
        parts.append(zb0[:, o + gr:o + 2 * gr] + zb1[:, o:o + gr])
    scat = jnp.concatenate(parts, axis=1)

    ey = lax.all_to_all(scat, BOTH, 0, 0, tiled=True)
    zz = mm(ey, wre, ((0,), (0,))).reshape(2, 2, g, r, 2 * by)
    vre = zz[:, 0, :, :, :by] - zz[:, 1, :, :, by:]
    vim = zz[:, 0, :, :, by:] + zz[:, 1, :, :, :by]
    vre2 = vre * c1[None, :, None, :] + vim * s1[None, :, None, :]
    vim2 = vim * c1[None, :, None, :] - vre * s1[None, :, None, :]
    vst = jnp.concatenate([vre2, vim2], axis=1).reshape(2, 2 * g, r * by)
    uv = mm(fy3, vst, ((1,), (1,))).reshape(g, 2, r, by)
    back = lax.all_to_all(uv, "gy", 0, 0, tiled=True)
    fields = jnp.concatenate([rows[:, None], uv], axis=1)
    sides = jnp.stack([jnp.roll(fields[:, :, :, -1], 1, axis=0),
                       jnp.roll(fields[:, :, :, 0], -1, axis=0)], axis=-1).reshape(g, 6 * r)
    sides = lax.all_to_all(sides, "gy", 0, 0, tiled=True).reshape(g, 3, r, 2)
    before = jnp.transpose(sides[..., 0], (1, 0, 2)).reshape(3, bx)
    after = jnp.transpose(sides[..., 1], (1, 0, 2)).reshape(3, bx)
    return back, before, after, n


def rate_kernel(k_ref, w_ref, back_ref, bot_ref, side_ref, frc_ref, out_ref, ext_ref):
    rows, cols = ext_ref.shape[1], ext_ref.shape[2]
    bx, by = out_ref.shape
    g, _, r, _ = back_ref.shape

    ext_ref[0, :bx, :by] = w_ref[...]
    for f in range(2):
        for j in range(g):
            ext_ref[1 + f, j * r:(j + 1) * r, :by] = back_ref[j, f]
    for c in range(3):
        ext_ref[c, bx:, :] = bot_ref[c]
        ext_ref[c, :bx, by:] = side_ref[c]

    def rr(a, s):
        return pltpu.roll(a, s % rows, 0)

    def lr(a, s):
        return pltpu.roll(a, s % cols, 1)

    w = ext_ref[0]
    u = ext_ref[1]
    v = ext_ref[2]
    wm = rr(w, 1)
    wp = rr(w, -1)
    ym = lr(w, 1)
    yp = lr(w, -1)
    adv = (jnp.maximum(u, 0.0) * (w - wm) + jnp.minimum(u, 0.0) * (wp - w)
           + jnp.maximum(v, 0.0) * (w - ym) + jnp.minimum(v, 0.0) * (yp - w))
    lap = wp + wm + yp + ym - 4.0 * w
    gs = [None, None, None]
    for c, f in enumerate((w, u, v)):
        fm = wm if c == 0 else rr(f, 1)
        fp = wp if c == 0 else rr(f, -1)
        for b in range(3):
            term = (k_ref[9 * c + b] * fm + k_ref[9 * c + 3 + b] * f
                    + k_ref[9 * c + 6 + b] * fp)
            gs[b] = term if gs[b] is None else gs[b] + term
    clo = gs[1] + lr(gs[0], 1) + lr(gs[2], -1)
    res = -adv + VISCOSITY * lap - DRAG * w + clo
    out_ref[...] = res[:bx, :by] + frc_ref[0:1, :]


def halo(top, bottom, left, right, corners):
    gx, gy = lax.axis_size("gx"), lax.axis_size("gy")

    def shift(x, axis, count, step):
        return lax.ppermute(x, axis, [(i, (i + step) % count) for i in range(count)])

    def diag(x, di, dj):
        pairs = []
        for i in range(gx):
            for j in range(gy):
                pairs.append((i * gy + j, ((i + di) % gx) * gy + (j + dj) % gy))
        return lax.ppermute(x, BOTH, pairs)

    below = shift(top, "gx", gx, -1)
    above = shift(bottom, "gx", gx, 1)
    after = shift(left, "gy", gy, -1)
    before = shift(right, "gy", gy, 1)
    c_br = diag(corners[:, 0], -1, -1)
    c_bl = diag(corners[:, 1], -1, 1)
    c_tr = diag(corners[:, 2], 1, -1)
    c_tl = diag(corners[:, 3], 1, 1)
    return below, above, after, before, c_br, c_bl, c_tr, c_tl


def strips(parts, bx, by, rows, cols):
    below, above, after, before, c_br, c_bl, c_tr, c_tl = parts
    nc = below.shape[0]
    ri = jnp.arange(rows - bx, dtype=jnp.int32)[:, None]
    ci = jnp.arange(cols, dtype=jnp.int32)[None, :]
    pad = cols - by
    row_lo = jnp.concatenate([below, c_br[:, None], jnp.zeros((nc, pad - 2)), c_bl[:, None]], axis=1)
    row_hi = jnp.concatenate([above, c_tr[:, None], jnp.zeros((nc, pad - 2)), c_tl[:, None]], axis=1)
    bot = jnp.where(ri[None] == 0, row_lo[:, None, :],
                    jnp.where(ri[None] == rows - bx - 1, row_hi[:, None, :], 0.0))
    si = jnp.arange(pad, dtype=jnp.int32)[None, None, :]
    side = jnp.where(si == 0, after[:, :, None], jnp.where(si == pad - 1, before[:, :, None], 0.0))
    return bot, side


def per_device(vorticity, closure_kernel):
    bx, by = vorticity.shape
    rows = -(-(bx + 2) // 8) * 8
    cols = -(-(by + 2) // 128) * 128
    w = vorticity
    back, before, after, n = velocity(vorticity)
    gx = lax.axis_size("gx")
    w = vorticity
    first = jnp.concatenate([w[None, 0], back[0, :, 0, :]], axis=0)
    last = jnp.concatenate([w[None, -1], back[-1, :, -1, :]], axis=0)
    top = jnp.concatenate([before[:, :1], first, after[:, :1]], axis=1)
    bottom = jnp.concatenate([before[:, -1:], last, after[:, -1:]], axis=1)
    below = lax.ppermute(top, "gx", [(i, (i - 1) % gx) for i in range(gx)])
    above = lax.ppermute(bottom, "gx", [(i, (i + 1) % gx) for i in range(gx)])
    parts = (below[:, 1:-1], above[:, 1:-1], after, before,
             below[:, -1], below[:, 0], above[:, -1], above[:, 0])
    bot, side = strips(parts, bx, by, rows, cols)
    columns = (lax.axis_index("gy") * by + jnp.arange(by, dtype=jnp.int32)).astype(jnp.float32)
    forcing = FORCE_AMP * jnp.cos(2.0 * math.pi * FORCE_WAVES / n * columns)
    frc = jnp.broadcast_to(forcing[None, :], (8, by))
    return pl.pallas_call(
        rate_kernel,
        out_shape=jax.ShapeDtypeStruct((bx, by), jnp.float32),
        in_specs=[pl.BlockSpec(memory_space=pltpu.SMEM)]
        + [pl.BlockSpec(memory_space=pltpu.VMEM)] * 5,
        out_specs=pl.BlockSpec(memory_space=pltpu.VMEM),
        scratch_shapes=[pltpu.VMEM((3, rows, cols), jnp.float32)],
        compiler_params=pltpu.CompilerParams(vmem_limit_bytes=60 * 1024 * 1024),
        cost_estimate=pl.CostEstimate(flops=60 * rows * cols, transcendentals=0,
                                      bytes_accessed=4 * (4 * rows * cols)),
    )(closure_kernel.reshape(-1), w, back, bot, side, frc)


def solution(mesh):
    placed = (P("gx", "gy"), P())
    return jax.shard_map(
        per_device, mesh=mesh, in_specs=placed, out_specs=P("gx", "gy"), check_vma=False
    )
```
